128 devices in a mesh: row: 8 (over x_lo, z), col: 16 (over y, x_hi, core).
Axes of the slice: x: 4 (x_hi: 2, x_lo: 2; x = x_hi * 2 + x_lo), y: 4, z: 4, core: 2. Of those that a mesh axis runs over, the one named last changes fastest.
Arguments:
- features: bfloat16 [32768, 512], P(('row', 'col')), may hold values from -6 to 6
- cotangent: bfloat16 [32768, 512], P(('row', 'col')), may hold values from -6 to 6
- weights: bfloat16 [512, 512], replicated, may hold values from -0.25 to 0.25
- bias_term: float32 [512], replicated, may hold values from -3 to 3
- adjacency: bfloat16 [8, 16, 128, 128, 128], P('row', 'col'), may hold values from -0.109375 to 0.109375
- tile_rows: int32 [8, 16, 128], P('row', 'col'), may hold values from 0 to 31, as said below
- tile_cols: int32 [8, 16, 128], P('row', 'col'), may hold values from 0 to 15
- tile_count: int32 [8, 16], P('row', 'col'), may hold values from 25 to 128, as said below
Outputs:
- activated: bfloat16 [32768, 512], P(('row', 'col'))
- grad_input: bfloat16 [32768, 512], P(('row', 'col'))
- grad_weight: float32 [512, 512], replicated
- grad_bias: float32 [512], replicated
The draws below stay inside these ranges and needn't reach their ends.
Inputs may be any that keep to these rules, and one draw needn't show every extreme that they name: Within one device the pairs (tile_rows, tile_cols) over all 128 slots are distinct. Only the first tile_count slots of a device are in use; some device uses all 128.
All inputs are finite; a program needn't handle non-finite values.
Results may differ from the reference program's by a relative error of at most 0.006.
Values may be sent and summed in bfloat16 or wider, within the bound.
No kernel may reach another device: no remote copies, remote signals or barrier semaphores. Data moves between devices by JAX's collectives and lax.ppermute only.
A program may use at most 128 MiB of HBM per device.

```python
import jax
import jax.numpy as jnp
from jax import lax

F = 512
TILE = 128
BPD = 2
TILE_CAP = 128
NODES = 32768
N_ROW = 8
N_COL = 16


def tile_pairs(key):
    pair_total = N_COL * BPD * N_ROW * BPD
    keys = jax.random.split(jax.random.fold_in(key, 11), N_ROW * N_COL)
    chosen = jax.vmap(lambda one_key: jax.random.permutation(one_key, pair_total)[:TILE_CAP])(keys)
    return chosen.reshape(N_ROW, N_COL, TILE_CAP).astype(jnp.int32)


def draw_tile_rows(key, part):
    return (tile_pairs(key) // (N_ROW * BPD)).astype(jnp.int32)


def draw_tile_cols(key, part):
    return (tile_pairs(key) % (N_ROW * BPD)).astype(jnp.int32)


def draw_tile_count(key, part):
    first_key = jax.random.fold_in(key, 23)
    second_key = jax.random.fold_in(key, 29)
    dev_total = N_ROW * N_COL
    low_count = max(1, TILE_CAP // 5)
    base_count = jax.random.randint(first_key, (dev_total,), low_count, TILE_CAP // 2 + 1, dtype=jnp.int32)
    busiest = jax.random.randint(second_key, (), 0, dev_total, dtype=jnp.int32)
    lightest = ((busiest + 1) % dev_total).astype(jnp.int32)
    base_count = base_count.at[lightest].set(low_count)
    base_count = base_count.at[busiest].set(TILE_CAP)
    return base_count.reshape(N_ROW, N_COL).astype(jnp.int32)


def level_of(own_key, shape, cuts, low, high):
    factor_of = 1.0
    for dim, parts in cuts:
        heights = jax.random.uniform(jax.random.fold_in(jax.random.fold_in(own_key, 6), dim), (parts,), jnp.float32, low / len(cuts), high / len(cuts))
        factor_of = factor_of * jnp.repeat(jnp.exp(heights), shape[dim] // parts).reshape((-1,) + (1,) * (len(shape) - 1 - dim))
    return factor_of


def bell_draw(own_key, shape, width, bound, pieces=(), kind=jnp.bfloat16):
    values = jax.random.normal(own_key, shape, jnp.float32) * width
    if len(pieces) > 0:
        values = level_of(own_key, shape, pieces, -0.22, 0.18) * values
    return jnp.clip(values, min=-bound, max=bound).astype(kind)


def setup_inputs(seed: int = 0) -> dict:
    streams_of = jax.random.split(jax.random.key(seed), 9)
    features = bell_draw(streams_of[0], (NODES, F), 1.0, 6.0, ((0, 128),))
    cotangent = bell_draw(streams_of[1], (NODES, F), 1.0, 6.0, ((0, 128),))
    weights = bell_draw(streams_of[2], (F, F), F ** -0.5, 0.25)
    bias_term = bell_draw(streams_of[3], (F,), 0.5, 3.0, (), jnp.float32)
    adjacency = bell_draw(streams_of[4], (N_ROW, N_COL, TILE_CAP, TILE, TILE), (TILE * TILE_CAP // (3 * BPD)) ** -0.5, 0.109375, ((0, 8), (1, 16)))
    tile_rows = draw_tile_rows(jax.random.fold_in(streams_of[8], 71), 0)
    tile_cols = draw_tile_cols(jax.random.fold_in(streams_of[8], 71), 0)
    tile_count = draw_tile_count(jax.random.fold_in(streams_of[8], 71), 0)
    return {"features": features, "cotangent": cotangent, "weights": weights, "bias_term": bias_term, "adjacency": adjacency, "tile_rows": tile_rows, "tile_cols": tile_cols, "tile_count": tile_count}


def global_ids(grid_row, grid_col, tile_rows, tile_cols):
    row_piece = grid_row * N_COL + tile_rows // BPD
    col_piece = (tile_cols // BPD) * N_COL + grid_col
    row_block = row_piece * BPD + tile_rows % BPD
    col_block = col_piece * BPD + tile_cols % BPD
    return row_block.astype(jnp.int32), col_block.astype(jnp.int32)


def reference(features, cotangent, weights, bias_term, adjacency, tile_rows, tile_cols, tile_count):
    block_total = NODES // TILE
    dev_total = N_ROW * N_COL
    grid_row = (jnp.arange(dev_total, dtype=jnp.int32) // N_COL).astype(jnp.int32)
    grid_col = (jnp.arange(dev_total, dtype=jnp.int32) % N_COL).astype(jnp.int32)
    flat_tiles = adjacency.reshape(dev_total, TILE_CAP, TILE, TILE)
    flat_rows = tile_rows.reshape(dev_total, TILE_CAP)
    flat_cols = tile_cols.reshape(dev_total, TILE_CAP)
    flat_count = tile_count.reshape(dev_total)
    slot_index = jnp.arange(TILE_CAP, dtype=jnp.int32)

    projected = jnp.dot(features, weights, preferred_element_type=jnp.float32).astype(jnp.bfloat16)
    proj_blocks = projected.reshape(block_total, TILE, F)

    def forward_step(carry, inputs):
        tile_data, rows_here, cols_here, count_here, row_here, col_here = inputs
        row_block, col_block = global_ids(row_here, col_here, rows_here, cols_here)
        in_use = (slot_index < count_here).astype(jnp.float32)
        picked = proj_blocks[col_block].astype(jnp.float32)
        products = jnp.einsum("tij,tjf->tif", tile_data.astype(jnp.float32), picked)
        products = products * in_use[:, None, None]
        return carry.at[row_block].add(products), None

    start_blocks = jnp.zeros((block_total, TILE, F), jnp.float32)
    summed, _ = lax.scan(forward_step, start_blocks, (flat_tiles, flat_rows, flat_cols, flat_count, grid_row, grid_col))
    summed = summed.reshape(NODES, F)
    shifted = summed + bias_term[None, :]
    activated = jax.nn.silu(shifted).astype(jnp.bfloat16)
    sig = jax.nn.sigmoid(shifted)
    slope = (cotangent.astype(jnp.float32) * sig * (1.0 + shifted * (1.0 - sig))).astype(jnp.bfloat16)
    slope_blocks = slope.reshape(block_total, TILE, F)

    def backward_step(carry, inputs):
        tile_data, rows_here, cols_here, count_here, row_here, col_here = inputs
        row_block, col_block = global_ids(row_here, col_here, rows_here, cols_here)
        in_use = (slot_index < count_here).astype(jnp.float32)
        picked = slope_blocks[row_block].astype(jnp.float32)
        products = jnp.einsum("tji,tjf->tif", tile_data.astype(jnp.float32), picked)
        products = products * in_use[:, None, None]
        return carry.at[col_block].add(products), None

    back, _ = lax.scan(backward_step, start_blocks, (flat_tiles, flat_rows, flat_cols, flat_count, grid_row, grid_col))
    back = back.reshape(NODES, F).astype(jnp.bfloat16)
    grad_input = jnp.dot(back, weights.T, preferred_element_type=jnp.float32).astype(jnp.bfloat16)
    node_scale = NODES ** -0.5
    grad_weight = jnp.dot(features.T, back, preferred_element_type=jnp.float32) * node_scale
    grad_bias = jnp.sum(slope.astype(jnp.float32), axis=0) * node_scale
    return activated, grad_input, grad_weight, grad_bias
```

```python
import math

import jax
import jax.numpy as jnp
from jax import lax
from jax.sharding import PartitionSpec as P


def dense_blocks(tile_data, row_ids, col_ids, in_count, row_total, col_total):
    slot_total, tile_size, _ = tile_data.shape
    slot_range = jnp.arange(slot_total, dtype=jnp.int32)
    pair_of = jnp.where(slot_range < in_count, row_ids * col_total + col_ids, -1)
    pair_range = jnp.arange(row_total * col_total, dtype=jnp.int32)
    onehot = (pair_range[:, None] == pair_of[None, :]).astype(tile_data.dtype)
    placed = jnp.dot(
        onehot,
        tile_data.reshape(slot_total, tile_size * tile_size),
        preferred_element_type=jnp.float32,
    ).astype(tile_data.dtype)
    return placed.reshape(row_total, col_total, tile_size, tile_size)


def slope_of(shifted, cotangent):
    sig = jax.nn.sigmoid(shifted)
    return (cotangent.astype(jnp.float32) * sig * (1.0 + shifted * (1.0 - sig))).astype(
        jnp.bfloat16
    )


def on_device(features, cotangent, weights, bias_term, adjacency, tile_rows, tile_cols, tile_count):
    tile_size = adjacency.shape[-1]
    slot_total = adjacency.shape[2]
    tile_data = adjacency.reshape(slot_total, tile_size, tile_size)
    row_ids = tile_rows.reshape(slot_total)
    col_ids = tile_cols.reshape(slot_total)
    in_count = tile_count.reshape(())
    n_row = lax.axis_size("row")
    n_col = lax.axis_size("col")
    own_rows = features.shape[0]
    own_blocks = own_rows // tile_size
    feat_width = features.shape[1]
    row_total = n_col * own_blocks
    col_total = n_row * own_blocks
    node_scale = 1.0 / math.sqrt(own_rows * n_row * n_col)

    dense = dense_blocks(tile_data, row_ids, col_ids, in_count, row_total, col_total)

    projected = jnp.dot(features, weights, preferred_element_type=jnp.float32).astype(jnp.bfloat16)
    gathered = lax.all_gather(projected, "row", axis=0, tiled=True)
    gathered = gathered.reshape(col_total, tile_size, feat_width)
    partial_rows = jnp.einsum(
        "rcij,cjf->rif", dense, gathered, preferred_element_type=jnp.float32
    ).reshape(row_total * tile_size, feat_width)
    bias_row = bias_term[None, :]
    shifted = lax.psum_scatter(partial_rows, "col", scatter_dimension=0, tiled=True) + bias_row
    slope_own = slope_of(shifted, cotangent)
    slope_rows = lax.all_gather(slope_own, "col", axis=0, tiled=True)
    slope_rows = slope_rows.reshape(row_total, tile_size, feat_width)
    activated = jax.nn.silu(shifted).astype(jnp.bfloat16)
    bias_part = jnp.sum(slope_own.astype(jnp.float32), axis=0)
    partial_cols = jnp.einsum(
        "rcij,rif->cjf", dense, slope_rows, preferred_element_type=jnp.float32
    ).reshape(col_total * tile_size, feat_width)
    back = lax.psum_scatter(partial_cols, "row", scatter_dimension=0, tiled=True).astype(
        jnp.bfloat16
    )
    grad_input = lax.dot_general(
        back, weights, (((1,), (1,)), ((), ())), preferred_element_type=jnp.float32
    ).astype(jnp.bfloat16)
    weight_part = lax.dot_general(
        features, back, (((0,), (0,)), ((), ())), preferred_element_type=jnp.float32
    )
    joined = jnp.concatenate([weight_part.reshape(-1), bias_part])
    joined = lax.psum(joined, ("row", "col"))
    weight_sum = joined[: feat_width * feat_width].reshape(feat_width, feat_width)
    bias_sum = joined[feat_width * feat_width :]
    return (activated, grad_input, weight_sum * node_scale, bias_sum * node_scale)


def solution(mesh):
    return jax.shard_map(
        on_device,
        mesh=mesh,
        in_specs=(
            P(("row", "col"), None),
            P(("row", "col"), None),
            P(),
            P(),
            P("row", "col", None, None, None),
            P("row", "col", None),
            P("row", "col", None),
            P("row", "col"),
        ),
        out_specs=(P(("row", "col"), None), P(("row", "col"), None), P(), P()),
        check_vma=False,
    )
```

```python
import math

import jax
import jax.numpy as jnp
from jax import lax
from jax.sharding import PartitionSpec as P


def dense_blocks(tile_data, row_ids, col_ids, in_count, row_total, col_total):
    slot_total, tile_size, _ = tile_data.shape
    slot_range = jnp.arange(slot_total, dtype=jnp.int32)
    pair_of = jnp.where(slot_range < in_count, row_ids * col_total + col_ids, -1)
    pair_range = jnp.arange(row_total * col_total, dtype=jnp.int32)
    onehot = (pair_range[:, None] == pair_of[None, :]).astype(tile_data.dtype)
    placed = jnp.dot(
        onehot,
        tile_data.reshape(slot_total, tile_size * tile_size),
        preferred_element_type=jnp.float32,
    ).astype(tile_data.dtype)
    return placed.reshape(row_total, col_total, tile_size, tile_size)


def gather_by_a2a(x, axis_name, n):
    spread = jnp.broadcast_to(x[None], (n,) + x.shape)
    return lax.all_to_all(spread, axis_name, 0, 0, tiled=False).reshape((n * x.shape[0],) + x.shape[1:])


def scatter_sum_by_a2a(x, axis_name, n, link_dtype):
    parts = x.astype(link_dtype).reshape((n, x.shape[0] // n) + x.shape[1:])
    got = lax.all_to_all(parts, axis_name, 0, 0, tiled=False)
    return jnp.sum(got.astype(jnp.float32), axis=0)


def all_sum_by_a2a(x, axis_names, n):
    pad = (-x.shape[0]) % n
    parts = jnp.pad(x, (0, pad)).reshape(n, -1)
    got = lax.all_to_all(parts, axis_names, 0, 0, tiled=False)
    mine = jnp.sum(got, axis=0)
    back = lax.all_to_all(jnp.broadcast_to(mine[None], parts.shape), axis_names, 0, 0, tiled=False)
    return back.reshape(-1)[: x.shape[0]]


def slope_of(shifted, cotangent):
    sig = jax.nn.sigmoid(shifted)
    return (cotangent.astype(jnp.float32) * sig * (1.0 + shifted * (1.0 - sig))).astype(
        jnp.bfloat16
    )


def on_device(features, cotangent, weights, bias_term, adjacency, tile_rows, tile_cols, tile_count):
    tile_size = adjacency.shape[-1]
    slot_total = adjacency.shape[2]
    tile_data = adjacency.reshape(slot_total, tile_size, tile_size)
    row_ids = tile_rows.reshape(slot_total)
    col_ids = tile_cols.reshape(slot_total)
    in_count = tile_count.reshape(())
    n_row = lax.axis_size("row")
    n_col = lax.axis_size("col")
    own_rows = features.shape[0]
    own_blocks = own_rows // tile_size
    feat_width = features.shape[1]
    row_total = n_col * own_blocks
    col_total = n_row * own_blocks
    node_scale = 1.0 / math.sqrt(own_rows * n_row * n_col)

    dense = dense_blocks(tile_data, row_ids, col_ids, in_count, row_total, col_total)

    projected = jnp.dot(features, weights, preferred_element_type=jnp.float32).astype(jnp.bfloat16)
    gathered = gather_by_a2a(projected, "row", n_row)
    gathered = gathered.reshape(col_total, tile_size, feat_width)
    partial_rows = jnp.einsum(
        "rcij,cjf->rif", dense, gathered, preferred_element_type=jnp.float32
    ).reshape(row_total * tile_size, feat_width)
    bias_row = bias_term[None, :]
    shifted = scatter_sum_by_a2a(partial_rows, "col", n_col, jnp.bfloat16) + bias_row
    slope_own = slope_of(shifted, cotangent)
    slope_rows = gather_by_a2a(slope_own, "col", n_col)
    slope_rows = slope_rows.reshape(row_total, tile_size, feat_width)
    activated = jax.nn.silu(shifted).astype(jnp.bfloat16)
    bias_part = jnp.sum(slope_own.astype(jnp.float32), axis=0)
    partial_cols = jnp.einsum(
        "rcij,rif->cjf", dense, slope_rows, preferred_element_type=jnp.float32
    ).reshape(col_total * tile_size, feat_width)
    back = scatter_sum_by_a2a(partial_cols, "row", n_row, jnp.bfloat16).astype(jnp.bfloat16)
    grad_input = lax.dot_general(
        back, weights, (((1,), (1,)), ((), ())), preferred_element_type=jnp.float32
    ).astype(jnp.bfloat16)
    weight_part = lax.dot_general(
        features, back, (((0,), (0,)), ((), ())), preferred_element_type=jnp.float32
    )
    joined = jnp.concatenate([weight_part.reshape(-1), bias_part])
    joined = all_sum_by_a2a(joined, ("row", "col"), n_row * n_col)
    weight_sum = joined[: feat_width * feat_width].reshape(feat_width, feat_width)
    bias_sum = joined[feat_width * feat_width :]
    return (activated, grad_input, weight_sum * node_scale, bias_sum * node_scale)


def solution(mesh):
    return jax.shard_map(
        on_device,
        mesh=mesh,
        in_specs=(
            P(("row", "col"), None),
            P(("row", "col"), None),
            P(),
            P(),
            P("row", "col", None, None, None),
            P("row", "col", None),
            P("row", "col", None),
            P("row", "col"),
        ),
        out_specs=(P(("row", "col"), None), P(("row", "col"), None), P(), P()),
        check_vma=False,
    )
```

```python
import math

import jax
import jax.numpy as jnp
from jax import lax
from jax.sharding import PartitionSpec as P


def col_parts(c):
    return c // 4, (c // 2) % 2, c % 2


def relative_col(c2, me):
    y2, x2, k2 = col_parts(c2)
    y1, x1, k1 = col_parts(me)
    return ((y2 - y1) % 4) * 4 + (x2 ^ x1) * 2 + (k2 ^ k1)


def col_perm(n, move):
    return [(c, move(c)) for c in range(n)]


def scatter_sum_col(parts, n):
    rest = parts.shape[1:]
    parts = parts.reshape((4, 2, 2) + rest)
    got = lax.ppermute(parts[:, :, 1], "col", col_perm(n, lambda c: c ^ 1))
    acc = parts[:, :, 0] + got
    total = acc[0]
    for shift in range(1, 4):
        sent = acc[shift].astype(jnp.bfloat16)
        got = lax.ppermute(sent, "col", col_perm(n, lambda c, s=shift: ((c // 4 + s) % 4) * 4 + c % 4))
        total = total + got.astype(jnp.float32)
    got = lax.ppermute(total[1], "col", col_perm(n, lambda c: c ^ 2))
    return total[0] + got


def gather_col(own, n):
    got = lax.ppermute(own, "col", col_perm(n, lambda c: c ^ 2))
    pair = jnp.stack([own, got])
    by_shift = [pair]
    for shift in (3, 2, 1):
        by_shift.append(
            lax.ppermute(pair, "col", col_perm(n, lambda c, s=shift: ((c // 4 + s) % 4) * 4 + c % 4))
        )
    quad = jnp.stack(by_shift)
    got = lax.ppermute(quad, "col", col_perm(n, lambda c: c ^ 1))
    full = jnp.stack([quad, got], axis=2)
    return full.reshape((16,) + own.shape)


def dense_blocks(tile_data, row_ids, col_ids, in_count, row_total, col_total):
    slot_total, tile_size, _ = tile_data.shape
    slot_range = jnp.arange(slot_total, dtype=jnp.int32)
    pair_of = jnp.where(slot_range < in_count, row_ids * col_total + col_ids, -1)
    pair_range = jnp.arange(row_total * col_total, dtype=jnp.int32)
    onehot = (pair_range[:, None] == pair_of[None, :]).astype(tile_data.dtype)
    placed = jnp.dot(
        onehot,
        tile_data.reshape(slot_total, tile_size * tile_size),
        preferred_element_type=jnp.float32,
    ).astype(tile_data.dtype)
    return placed.reshape(row_total, col_total, tile_size, tile_size)


def gather_by_a2a(x, axis_name, n):
    spread = jnp.broadcast_to(x[None], (n,) + x.shape)
    return lax.all_to_all(spread, axis_name, 0, 0, tiled=False).reshape((n * x.shape[0],) + x.shape[1:])


def scatter_sum_by_a2a(x, axis_name, n, link_dtype):
    parts = x.astype(link_dtype).reshape((n, x.shape[0] // n) + x.shape[1:])
    got = lax.all_to_all(parts, axis_name, 0, 0, tiled=False)
    return jnp.sum(got.astype(jnp.float32), axis=0)


def all_sum_by_a2a(x, axis_names, n):
    pad = (-x.shape[0]) % n
    parts = jnp.pad(x, (0, pad)).reshape(n, -1)
    got = lax.all_to_all(parts, axis_names, 0, 0, tiled=False)
    mine = jnp.sum(got, axis=0)
    back = lax.all_to_all(jnp.broadcast_to(mine[None], parts.shape), axis_names, 0, 0, tiled=False)
    return back.reshape(-1)[: x.shape[0]]


def slope_of(shifted, cotangent):
    sig = jax.nn.sigmoid(shifted)
    return (cotangent.astype(jnp.float32) * sig * (1.0 + shifted * (1.0 - sig))).astype(
        jnp.bfloat16
    )


def on_device(features, cotangent, weights, bias_term, adjacency, tile_rows, tile_cols, tile_count):
    tile_size = adjacency.shape[-1]
    slot_total = adjacency.shape[2]
    tile_data = adjacency.reshape(slot_total, tile_size, tile_size)
    row_ids = tile_rows.reshape(slot_total)
    col_ids = tile_cols.reshape(slot_total)
    in_count = tile_count.reshape(())
    n_row = lax.axis_size("row")
    n_col = lax.axis_size("col")
    own_rows = features.shape[0]
    own_blocks = own_rows // tile_size
    feat_width = features.shape[1]
    row_total = n_col * own_blocks
    col_total = n_row * own_blocks
    node_scale = 1.0 / math.sqrt(own_rows * n_row * n_col)

    me_col = lax.axis_index("col")
    rel_rows = relative_col(row_ids // own_blocks, me_col) * own_blocks + row_ids % own_blocks
    dense = dense_blocks(tile_data, rel_rows, col_ids, in_count, row_total, col_total)

    projected = jnp.dot(features, weights, preferred_element_type=jnp.float32).astype(jnp.bfloat16)
    gathered = gather_by_a2a(projected, "row", n_row)
    gathered = gathered.reshape(col_total, tile_size, feat_width)
    partial_rows = jnp.einsum(
        "rcij,cjf->rif", dense, gathered, preferred_element_type=jnp.float32
    ).reshape(row_total * tile_size, feat_width)
    bias_row = bias_term[None, :]
    shifted = scatter_sum_col(partial_rows.reshape(n_col, own_rows, feat_width), n_col) + bias_row
    slope_own = slope_of(shifted, cotangent)
    slope_rows = gather_col(slope_own, n_col)
    slope_rows = slope_rows.reshape(row_total, tile_size, feat_width)
    activated = jax.nn.silu(shifted).astype(jnp.bfloat16)
    bias_part = jnp.sum(slope_own.astype(jnp.float32), axis=0)
    partial_cols = jnp.einsum(
        "rcij,rif->cjf", dense, slope_rows, preferred_element_type=jnp.float32
    ).reshape(col_total * tile_size, feat_width)
    back = scatter_sum_by_a2a(partial_cols, "row", n_row, jnp.bfloat16).astype(jnp.bfloat16)
    grad_input = lax.dot_general(
        back, weights, (((1,), (1,)), ((), ())), preferred_element_type=jnp.float32
    ).astype(jnp.bfloat16)
    weight_part = lax.dot_general(
        features, back, (((0,), (0,)), ((), ())), preferred_element_type=jnp.float32
    )
    dev_total = n_row * n_col
    pack_rows = -(-(feat_width + 1) // dev_total)
    joined = jnp.concatenate(
        [weight_part, bias_part[None, :],
         jnp.zeros((pack_rows * dev_total - feat_width - 1, feat_width), jnp.float32)]
    ).reshape(dev_total, pack_rows, feat_width)
    got = lax.all_to_all(joined, ("row", "col"), 0, 0, tiled=False)
    mine = jnp.sum(got, axis=0)
    joined = lax.all_to_all(
        jnp.broadcast_to(mine[None], joined.shape), ("row", "col"), 0, 0, tiled=False
    ).reshape(dev_total * pack_rows, feat_width)
    weight_sum = joined[:feat_width]
    bias_sum = joined[feat_width]
    return (activated, grad_input, weight_sum * node_scale, bias_sum * node_scale)


def solution(mesh):
    return jax.shard_map(
        on_device,
        mesh=mesh,
        in_specs=(
            P(("row", "col"), None),
            P(("row", "col"), None),
            P(),
            P(),
            P("row", "col", None, None, None),
            P("row", "col", None),
            P("row", "col", None),
            P("row", "col"),
        ),
        out_specs=(P(("row", "col"), None), P(("row", "col"), None), P(), P()),
        check_vma=False,
    )
```

```python
import math

import jax
import jax.numpy as jnp
from jax import lax
from jax.experimental import pallas as pl
from jax.experimental.pallas import tpu as pltpu
from jax.sharding import PartitionSpec as P


def place_kernel(slot_ref, adj_ref, dense_ref, dense_t_ref):
    row = pl.program_id(0)
    col_total = dense_ref.shape[1] // adj_ref.shape[-1]
    size = adj_ref.shape[-1]
    for col in range(col_total):
        slot = slot_ref[row * col_total + col]
        tile = adj_ref[jnp.maximum(slot, 0)]
        tile = jnp.where(slot >= 0, tile, jnp.zeros_like(tile))
        dense_ref[:, col * size : (col + 1) * size] = tile
        dense_t_ref[col * size : (col + 1) * size, :] = tile.T


def dense_blocks(tile_data, row_ids, col_ids, in_count, row_total, col_total):
    slot_total, size, _ = tile_data.shape
    slot_range = jnp.arange(slot_total, dtype=jnp.int32)
    pair_of = jnp.where(slot_range < in_count, row_ids * col_total + col_ids, -1)
    pair_range = jnp.arange(row_total * col_total, dtype=jnp.int32)
    slot_of = jnp.max(
        jnp.where(pair_range[:, None] == pair_of[None, :], slot_range[None, :], -1), axis=1
    )
    return pl.pallas_call(
        place_kernel,
        grid_spec=pltpu.PrefetchScalarGridSpec(
            num_scalar_prefetch=1,
            grid=(row_total,),
            in_specs=[pl.BlockSpec((slot_total, size, size), lambda r, slots: (0, 0, 0))],
            out_specs=[
                pl.BlockSpec((size, col_total * size), lambda r, slots: (r, 0)),
                pl.BlockSpec((col_total * size, size), lambda r, slots: (0, r)),
            ],
        ),
        out_shape=[
            jax.ShapeDtypeStruct((row_total * size, col_total * size), tile_data.dtype),
            jax.ShapeDtypeStruct((col_total * size, row_total * size), tile_data.dtype),
        ],
        compiler_params=pltpu.CompilerParams(vmem_limit_bytes=48 * 1024 * 1024),
        cost_estimate=pl.CostEstimate(
            flops=0,
            transcendentals=0,
            bytes_accessed=slot_total * size * size * 2 + 2 * row_total * col_total * size * size * 2,
        ),
    )(slot_of, tile_data)


def gather_by_a2a(x, axis_name, n):
    spread = jnp.broadcast_to(x[None], (n,) + x.shape)
    return lax.all_to_all(spread, axis_name, 0, 0, tiled=False).reshape((n * x.shape[0],) + x.shape[1:])


def scatter_sum_by_a2a(x, axis_name, n, link_dtype):
    parts = x.astype(link_dtype).reshape((n, x.shape[0] // n) + x.shape[1:])
    got = lax.all_to_all(parts, axis_name, 0, 0, tiled=False)
    return jnp.sum(got.astype(jnp.float32), axis=0)


def all_sum_by_a2a(x, axis_names, n):
    pad = (-x.shape[0]) % n
    parts = jnp.pad(x, (0, pad)).reshape(n, -1)
    got = lax.all_to_all(parts, axis_names, 0, 0, tiled=False)
    mine = jnp.sum(got, axis=0)
    back = lax.all_to_all(jnp.broadcast_to(mine[None], parts.shape), axis_names, 0, 0, tiled=False)
    return back.reshape(-1)[: x.shape[0]]


def slope_of(shifted, cotangent):
    sig = jax.nn.sigmoid(shifted)
    return (cotangent.astype(jnp.float32) * sig * (1.0 + shifted * (1.0 - sig))).astype(
        jnp.bfloat16
    )


def on_device(features, cotangent, weights, bias_term, adjacency, tile_rows, tile_cols, tile_count):
    tile_size = adjacency.shape[-1]
    slot_total = adjacency.shape[2]
    tile_data = adjacency.reshape(slot_total, tile_size, tile_size)
    row_ids = tile_rows.reshape(slot_total)
    col_ids = tile_cols.reshape(slot_total)
    in_count = tile_count.reshape(())
    n_row = lax.axis_size("row")
    n_col = lax.axis_size("col")
    own_rows = features.shape[0]
    own_blocks = own_rows // tile_size
    feat_width = features.shape[1]
    row_total = n_col * own_blocks
    col_total = n_row * own_blocks
    node_scale = 1.0 / math.sqrt(own_rows * n_row * n_col)

    dense, dense_t = dense_blocks(tile_data, row_ids, col_ids, in_count, row_total, col_total)

    projected = jnp.dot(features, weights, preferred_element_type=jnp.float32).astype(jnp.bfloat16)
    gathered = gather_by_a2a(projected, "row", n_row)
    partial_rows = jnp.dot(dense, gathered, preferred_element_type=jnp.float32)
    bias_row = bias_term[None, :]
    shifted = scatter_sum_by_a2a(partial_rows, "col", n_col, jnp.bfloat16) + bias_row
    slope_own = slope_of(shifted, cotangent)
    slope_rows = gather_by_a2a(slope_own, "col", n_col)
    activated = jax.nn.silu(shifted).astype(jnp.bfloat16)
    bias_part = jnp.sum(slope_own.astype(jnp.float32), axis=0)
    partial_cols = jnp.dot(dense_t, slope_rows, preferred_element_type=jnp.float32)
    back = scatter_sum_by_a2a(partial_cols, "row", n_row, jnp.bfloat16).astype(jnp.bfloat16)
    grad_input = lax.dot_general(
        back, weights, (((1,), (1,)), ((), ())), preferred_element_type=jnp.float32
    ).astype(jnp.bfloat16)
    weight_part = lax.dot_general(
        features, back, (((0,), (0,)), ((), ())), preferred_element_type=jnp.float32
    )
    joined = jnp.concatenate([weight_part.reshape(-1), bias_part])
    joined = all_sum_by_a2a(joined, ("row", "col"), n_row * n_col)
    weight_sum = joined[: feat_width * feat_width].reshape(feat_width, feat_width)
    bias_sum = joined[feat_width * feat_width :]
    return (activated, grad_input, weight_sum * node_scale, bias_sum * node_scale)


def solution(mesh):
    return jax.shard_map(
        on_device,
        mesh=mesh,
        in_specs=(
            P(("row", "col"), None),
            P(("row", "col"), None),
            P(),
            P(),
            P("row", "col", None, None, None),
            P("row", "col", None),
            P("row", "col", None),
            P("row", "col"),
        ),
        out_specs=(P(("row", "col"), None), P(("row", "col"), None), P(), P()),
        check_vma=False,
    )
```

```python
import math

import jax
import jax.numpy as jnp
from jax import lax
from jax.experimental import pallas as pl
from jax.experimental.pallas import tpu as pltpu
from jax.sharding import PartitionSpec as P


def place_kernel(slot_ref, adj_ref, dense_ref, dense_t_ref):
    row = pl.program_id(0)
    col_total = dense_ref.shape[1] // adj_ref.shape[-1]
    size = adj_ref.shape[-1]
    for col in range(col_total):
        slot = slot_ref[row * col_total + col]
        tile = adj_ref[jnp.maximum(slot, 0)]
        tile = jnp.where(slot >= 0, tile, jnp.zeros_like(tile))
        dense_ref[:, col * size : (col + 1) * size] = tile
        dense_t_ref[col * size : (col + 1) * size, :] = tile.T


def dense_blocks(tile_data, row_ids, col_ids, in_count, row_total, col_total):
    slot_total, size, _ = tile_data.shape
    slot_range = jnp.arange(slot_total, dtype=jnp.int32)
    pair_of = jnp.where(slot_range < in_count, row_ids * col_total + col_ids, -1)
    pair_range = jnp.arange(row_total * col_total, dtype=jnp.int32)
    slot_of = jnp.max(
        jnp.where(pair_range[:, None] == pair_of[None, :], slot_range[None, :], -1), axis=1
    )
    return pl.pallas_call(
        place_kernel,
        grid_spec=pltpu.PrefetchScalarGridSpec(
            num_scalar_prefetch=1,
            grid=(row_total,),
            in_specs=[pl.BlockSpec((slot_total, size, size), lambda r, slots: (0, 0, 0))],
            out_specs=[
                pl.BlockSpec((size, col_total * size), lambda r, slots: (r, 0)),
                pl.BlockSpec((col_total * size, size), lambda r, slots: (0, r)),
            ],
        ),
        out_shape=[
            jax.ShapeDtypeStruct((row_total * size, col_total * size), tile_data.dtype),
            jax.ShapeDtypeStruct((col_total * size, row_total * size), tile_data.dtype),
        ],
        compiler_params=pltpu.CompilerParams(vmem_limit_bytes=48 * 1024 * 1024),
        cost_estimate=pl.CostEstimate(
            flops=0,
            transcendentals=0,
            bytes_accessed=slot_total * size * size * 2 + 2 * row_total * col_total * size * size * 2,
        ),
    )(slot_of, tile_data)


def gather_by_a2a(x, axis_name, n):
    spread = jnp.broadcast_to(x[None], (n,) + x.shape)
    return lax.all_to_all(spread, axis_name, 0, 0, tiled=False).reshape((n * x.shape[0],) + x.shape[1:])


def scatter_sum_by_a2a(x, axis_name, n, link_dtype):
    parts = x.astype(link_dtype).reshape((n, x.shape[0] // n) + x.shape[1:])
    got = lax.all_to_all(parts, axis_name, 0, 0, tiled=False)
    return jnp.sum(got.astype(jnp.float32), axis=0)


def all_sum_by_a2a(x, axis_names, n):
    pad = (-x.shape[0]) % n
    parts = jnp.pad(x, (0, pad)).reshape(n, -1)
    got = lax.all_to_all(parts, axis_names, 0, 0, tiled=False)
    mine = jnp.sum(got, axis=0)
    back = lax.all_to_all(jnp.broadcast_to(mine[None], parts.shape), axis_names, 0, 0, tiled=False)
    return back.reshape(-1)[: x.shape[0]]


def slope_of(shifted, cotangent):
    sig = jax.nn.sigmoid(shifted)
    return (cotangent.astype(jnp.float32) * sig * (1.0 + shifted * (1.0 - sig))).astype(
        jnp.bfloat16
    )


def on_device(features, cotangent, weights, bias_term, adjacency, tile_rows, tile_cols, tile_count):
    tile_size = adjacency.shape[-1]
    slot_total = adjacency.shape[2]
    tile_data = adjacency.reshape(slot_total, tile_size, tile_size)
    row_ids = tile_rows.reshape(slot_total)
    col_ids = tile_cols.reshape(slot_total)
    in_count = tile_count.reshape(())
    n_row = lax.axis_size("row")
    n_col = lax.axis_size("col")
    own_rows = features.shape[0]
    own_blocks = own_rows // tile_size
    feat_width = features.shape[1]
    row_total = n_col * own_blocks
    col_total = n_row * own_blocks
    node_scale = 1.0 / math.sqrt(own_rows * n_row * n_col)

    dense, dense_t = dense_blocks(tile_data, row_ids, col_ids, in_count, row_total, col_total)

    chunks = 2
    chunk = feat_width // chunks
    bias_row = bias_term[None, :]
    activated_parts, back_parts, bias_parts = [], [], []
    for h in range(chunks):
        cols_h = slice(h * chunk, (h + 1) * chunk)
        projected = jnp.dot(
            features, weights[:, cols_h], preferred_element_type=jnp.float32
        ).astype(jnp.bfloat16)
        gathered = gather_by_a2a(projected, "row", n_row)
        partial_rows = jnp.dot(dense, gathered, preferred_element_type=jnp.float32)
        shifted = scatter_sum_by_a2a(partial_rows, "col", n_col, jnp.bfloat16) + bias_row[:, cols_h]
        slope_own = slope_of(shifted, cotangent[:, cols_h])
        slope_rows = gather_by_a2a(slope_own, "col", n_col)
        activated_parts.append(jax.nn.silu(shifted).astype(jnp.bfloat16))
        bias_parts.append(jnp.sum(slope_own.astype(jnp.float32), axis=0))
        partial_cols = jnp.dot(dense_t, slope_rows, preferred_element_type=jnp.float32)
        back_parts.append(
            scatter_sum_by_a2a(partial_cols, "row", n_row, jnp.bfloat16).astype(jnp.bfloat16)
        )
    activated = jnp.concatenate(activated_parts, axis=1)
    back = jnp.concatenate(back_parts, axis=1)
    bias_part = jnp.concatenate(bias_parts)
    grad_input = lax.dot_general(
        back, weights, (((1,), (1,)), ((), ())), preferred_element_type=jnp.float32
    ).astype(jnp.bfloat16)
    weight_part = lax.dot_general(
        features, back, (((0,), (0,)), ((), ())), preferred_element_type=jnp.float32
    )
    joined = jnp.concatenate([weight_part.reshape(-1), bias_part])
    joined = all_sum_by_a2a(joined, ("row", "col"), n_row * n_col)
    weight_sum = joined[: feat_width * feat_width].reshape(feat_width, feat_width)
    bias_sum = joined[feat_width * feat_width :]
    return (activated, grad_input, weight_sum * node_scale, bias_sum * node_scale)


def solution(mesh):
    return jax.shard_map(
        on_device,
        mesh=mesh,
        in_specs=(
            P(("row", "col"), None),
            P(("row", "col"), None),
            P(),
            P(),
            P("row", "col", None, None, None),
            P("row", "col", None),
            P("row", "col", None),
            P("row", "col"),
        ),
        out_specs=(P(("row", "col"), None), P(("row", "col"), None), P(), P()),
        check_vma=False,
    )
```

```python
import math

import jax
import jax.numpy as jnp
from jax import lax
from jax.experimental import pallas as pl
from jax.experimental.pallas import tpu as pltpu
from jax.sharding import PartitionSpec as P


def col_parts(c):
    return c // 4, (c // 2) % 2, c % 2


def relative_col(c2, me):
    y2, x2, k2 = col_parts(c2)
    y1, x1, k1 = col_parts(me)
    return ((y2 - y1) % 4) * 4 + (x2 ^ x1) * 2 + (k2 ^ k1)


def col_send(x, n, move):
    return lax.ppermute(x, "col", [(c, move(c)) for c in range(n)])


def y_up(c):
    return ((c // 4 + 1) % 4) * 4 + c % 4


def y_down(c):
    return ((c // 4 + 3) % 4) * 4 + c % 4


def scatter_sum_col(parts, n):
    rest = parts.shape[1:]
    parts = parts.reshape((4, 2, 2) + rest)
    acc = parts[:, :, 0] + col_send(parts[:, :, 1], n, lambda c: c ^ 1)
    via_up = col_send(acc[2, 0], n, y_up)
    via_down = col_send(acc[2, 1], n, y_down)
    to_up = jnp.stack([acc[1, 0] + via_up, acc[1, 1]]).astype(jnp.bfloat16)
    to_down = jnp.stack([acc[3, 0], acc[3, 1] + via_down]).astype(jnp.bfloat16)
    total = (
        acc[0]
        + col_send(to_up, n, y_up).astype(jnp.float32)
        + col_send(to_down, n, y_down).astype(jnp.float32)
    )
    return total[0] + col_send(total[1], n, lambda c: c ^ 2)


def gather_col(own, n):
    pair = jnp.stack([own, col_send(own, n, lambda c: c ^ 2)])
    from_below = col_send(pair, n, y_up)
    from_above = col_send(pair, n, y_down)
    two_away = jnp.stack([col_send(from_above[0], n, y_down), col_send(from_below[1], n, y_up)])
    quad = jnp.stack([pair, from_above, two_away, from_below])
    full = jnp.stack([quad, col_send(quad, n, lambda c: c ^ 1)], axis=2)
    return full.reshape((16,) + own.shape)


def place_kernel(slot_ref, adj_ref, dense_ref, dense_t_ref):
    row = pl.program_id(0)
    col_total = dense_ref.shape[1] // adj_ref.shape[-1]
    size = adj_ref.shape[-1]
    for col in range(col_total):
        slot = slot_ref[row * col_total + col]
        tile = adj_ref[jnp.maximum(slot, 0)]
        tile = jnp.where(slot >= 0, tile, jnp.zeros_like(tile))
        dense_ref[:, col * size : (col + 1) * size] = tile
        dense_t_ref[col * size : (col + 1) * size, :] = tile.T


def dense_blocks(tile_data, row_ids, col_ids, in_count, row_total, col_total):
    slot_total, size, _ = tile_data.shape
    slot_range = jnp.arange(slot_total, dtype=jnp.int32)
    pair_of = jnp.where(slot_range < in_count, row_ids * col_total + col_ids, -1)
    pair_range = jnp.arange(row_total * col_total, dtype=jnp.int32)
    slot_of = jnp.max(
        jnp.where(pair_range[:, None] == pair_of[None, :], slot_range[None, :], -1), axis=1
    )
    return pl.pallas_call(
        place_kernel,
        grid_spec=pltpu.PrefetchScalarGridSpec(
            num_scalar_prefetch=1,
            grid=(row_total,),
            in_specs=[pl.BlockSpec((slot_total, size, size), lambda r, slots: (0, 0, 0))],
            out_specs=[
                pl.BlockSpec((size, col_total * size), lambda r, slots: (r, 0)),
                pl.BlockSpec((col_total * size, size), lambda r, slots: (0, r)),
            ],
        ),
        out_shape=[
            jax.ShapeDtypeStruct((row_total * size, col_total * size), tile_data.dtype),
            jax.ShapeDtypeStruct((col_total * size, row_total * size), tile_data.dtype),
        ],
        compiler_params=pltpu.CompilerParams(vmem_limit_bytes=48 * 1024 * 1024),
        cost_estimate=pl.CostEstimate(
            flops=0,
            transcendentals=0,
            bytes_accessed=slot_total * size * size * 2 + 2 * row_total * col_total * size * size * 2,
        ),
    )(slot_of, tile_data)


def gather_by_a2a(x, axis_name, n):
    spread = jnp.broadcast_to(x[None], (n,) + x.shape)
    return lax.all_to_all(spread, axis_name, 0, 0, tiled=False).reshape((n * x.shape[0],) + x.shape[1:])


def scatter_sum_by_a2a(x, axis_name, n, link_dtype):
    parts = x.astype(link_dtype).reshape((n, x.shape[0] // n) + x.shape[1:])
    got = lax.all_to_all(parts, axis_name, 0, 0, tiled=False)
    return jnp.sum(got.astype(jnp.float32), axis=0)


def all_sum_by_a2a(x, axis_names, n):
    pad = (-x.shape[0]) % n
    parts = jnp.pad(x, (0, pad)).reshape(n, -1)
    got = lax.all_to_all(parts, axis_names, 0, 0, tiled=False)
    mine = jnp.sum(got, axis=0)
    back = lax.all_to_all(jnp.broadcast_to(mine[None], parts.shape), axis_names, 0, 0, tiled=False)
    return back.reshape(-1)[: x.shape[0]]


def slope_of(shifted, cotangent):
    sig = jax.nn.sigmoid(shifted)
    return (cotangent.astype(jnp.float32) * sig * (1.0 + shifted * (1.0 - sig))).astype(
        jnp.bfloat16
    )


def on_device(features, cotangent, weights, bias_term, adjacency, tile_rows, tile_cols, tile_count):
    tile_size = adjacency.shape[-1]
    slot_total = adjacency.shape[2]
    tile_data = adjacency.reshape(slot_total, tile_size, tile_size)
    row_ids = tile_rows.reshape(slot_total)
    col_ids = tile_cols.reshape(slot_total)
    in_count = tile_count.reshape(())
    n_row = lax.axis_size("row")
    n_col = lax.axis_size("col")
    own_rows = features.shape[0]
    own_blocks = own_rows // tile_size
    feat_width = features.shape[1]
    row_total = n_col * own_blocks
    col_total = n_row * own_blocks
    node_scale = 1.0 / math.sqrt(own_rows * n_row * n_col)

    me_col = lax.axis_index("col")
    rel_rows = relative_col(row_ids // own_blocks, me_col) * own_blocks + row_ids % own_blocks
    dense, dense_t = dense_blocks(tile_data, rel_rows, col_ids, in_count, row_total, col_total)

    projected = jnp.dot(features, weights, preferred_element_type=jnp.float32).astype(jnp.bfloat16)
    gathered = gather_by_a2a(projected, "row", n_row)
    partial_rows = jnp.dot(dense, gathered, preferred_element_type=jnp.float32)
    bias_row = bias_term[None, :]
    shifted = scatter_sum_col(partial_rows.reshape(n_col, own_rows, feat_width), n_col) + bias_row
    slope_own = slope_of(shifted, cotangent)
    slope_rows = gather_col(slope_own, n_col).reshape(n_col * own_rows, feat_width)
    activated = jax.nn.silu(shifted).astype(jnp.bfloat16)
    bias_part = jnp.sum(slope_own.astype(jnp.float32), axis=0)
    partial_cols = jnp.dot(dense_t, slope_rows, preferred_element_type=jnp.float32)
    back = scatter_sum_by_a2a(partial_cols, "row", n_row, jnp.bfloat16).astype(jnp.bfloat16)
    grad_input = lax.dot_general(
        back, weights, (((1,), (1,)), ((), ())), preferred_element_type=jnp.float32
    ).astype(jnp.bfloat16)
    weight_part = lax.dot_general(
        features, back, (((0,), (0,)), ((), ())), preferred_element_type=jnp.float32
    )
    joined = jnp.concatenate([weight_part.reshape(-1), bias_part])
    joined = all_sum_by_a2a(joined, ("row", "col"), n_row * n_col)
    weight_sum = joined[: feat_width * feat_width].reshape(feat_width, feat_width)
    bias_sum = joined[feat_width * feat_width :]
    return (activated, grad_input, weight_sum * node_scale, bias_sum * node_scale)


def solution(mesh):
    return jax.shard_map(
        on_device,
        mesh=mesh,
        in_specs=(
            P(("row", "col"), None),
            P(("row", "col"), None),
            P(),
            P(),
            P("row", "col", None, None, None),
            P("row", "col", None),
            P("row", "col", None),
            P("row", "col"),
        ),
        out_specs=(P(("row", "col"), None), P(("row", "col"), None), P(), P()),
        check_vma=False,
    )
```

```python
import math

import jax
import jax.numpy as jnp
from jax import lax
from jax.experimental import pallas as pl
from jax.experimental.pallas import tpu as pltpu
from jax.sharding import PartitionSpec as P


def col_parts(c):
    return c // 4, (c // 2) % 2, c % 2


def relative_col(c2, me):
    y2, x2, k2 = col_parts(c2)
    y1, x1, k1 = col_parts(me)
    return ((y2 - y1) % 4) * 4 + (x2 ^ x1) * 2 + (k2 ^ k1)


def col_send(x, n, move):
    return lax.ppermute(x, "col", [(c, move(c)) for c in range(n)])


def y_up(c):
    return ((c // 4 + 1) % 4) * 4 + c % 4


def y_down(c):
    return ((c // 4 + 3) % 4) * 4 + c % 4


def scatter_sum_col(parts, n):
    rest = parts.shape[1:]
    parts = parts.reshape((4, 2, 2) + rest)
    acc = parts[:, :, 0] + col_send(parts[:, :, 1], n, lambda c: c ^ 1)
    via_up = col_send(acc[2, 0].astype(jnp.bfloat16), n, y_up).astype(jnp.float32)
    via_down = col_send(acc[2, 1].astype(jnp.bfloat16), n, y_down).astype(jnp.float32)
    to_up = jnp.stack([acc[1, 0] + via_up, acc[1, 1]]).astype(jnp.bfloat16)
    to_down = jnp.stack([acc[3, 0], acc[3, 1] + via_down]).astype(jnp.bfloat16)
    total = (
        acc[0]
        + col_send(to_up, n, y_up).astype(jnp.float32)
        + col_send(to_down, n, y_down).astype(jnp.float32)
    )
    return total[0] + col_send(total[1].astype(jnp.bfloat16), n, lambda c: c ^ 2).astype(jnp.float32)


def gather_col(own, n):
    pair = jnp.stack([own, col_send(own, n, lambda c: c ^ 2)])
    from_below = col_send(pair, n, y_up)
    from_above = col_send(pair, n, y_down)
    two_away = jnp.stack([col_send(from_above[0], n, y_down), col_send(from_below[1], n, y_up)])
    quad = jnp.stack([pair, from_above, two_away, from_below])
    full = jnp.stack([quad, col_send(quad, n, lambda c: c ^ 1)], axis=2)
    return full.reshape((16,) + own.shape)


def place_kernel(slot_ref, adj_ref, dense_ref, dense_t_ref):
    row = pl.program_id(0)
    col_total = dense_ref.shape[1] // adj_ref.shape[-1]
    size = adj_ref.shape[-1]
    for col in range(col_total):
        slot = slot_ref[row * col_total + col]
        tile = adj_ref[jnp.maximum(slot, 0)]
        tile = jnp.where(slot >= 0, tile, jnp.zeros_like(tile))
        dense_ref[:, col * size : (col + 1) * size] = tile
        dense_t_ref[col * size : (col + 1) * size, :] = tile.T


def dense_blocks(tile_data, row_ids, col_ids, in_count, row_total, col_total):
    slot_total, size, _ = tile_data.shape
    slot_range = jnp.arange(slot_total, dtype=jnp.int32)
    pair_of = jnp.where(slot_range < in_count, row_ids * col_total + col_ids, -1)
    pair_range = jnp.arange(row_total * col_total, dtype=jnp.int32)
    slot_of = jnp.max(
        jnp.where(pair_range[:, None] == pair_of[None, :], slot_range[None, :], -1), axis=1
    )
    return pl.pallas_call(
        place_kernel,
        grid_spec=pltpu.PrefetchScalarGridSpec(
            num_scalar_prefetch=1,
            grid=(row_total,),
            in_specs=[pl.BlockSpec((slot_total, size, size), lambda r, slots: (0, 0, 0))],
            out_specs=[
                pl.BlockSpec((size, col_total * size), lambda r, slots: (r, 0)),
                pl.BlockSpec((col_total * size, size), lambda r, slots: (0, r)),
            ],
        ),
        out_shape=[
            jax.ShapeDtypeStruct((row_total * size, col_total * size), tile_data.dtype),
            jax.ShapeDtypeStruct((col_total * size, row_total * size), tile_data.dtype),
        ],
        compiler_params=pltpu.CompilerParams(vmem_limit_bytes=48 * 1024 * 1024),
        cost_estimate=pl.CostEstimate(
            flops=0,
            transcendentals=0,
            bytes_accessed=slot_total * size * size * 2 + 2 * row_total * col_total * size * size * 2,
        ),
    )(slot_of, tile_data)


def gather_by_a2a(x, axis_name, n):
    spread = jnp.broadcast_to(x[None], (n,) + x.shape)
    return lax.all_to_all(spread, axis_name, 0, 0, tiled=False).reshape((n * x.shape[0],) + x.shape[1:])


def scatter_sum_by_a2a(x, axis_name, n, link_dtype):
    parts = x.astype(link_dtype).reshape((n, x.shape[0] // n) + x.shape[1:])
    got = lax.all_to_all(parts, axis_name, 0, 0, tiled=False)
    return jnp.sum(got.astype(jnp.float32), axis=0)


def all_sum_by_a2a(x, axis_names, n, scale):
    pad = (-x.shape[0]) % n
    parts = jnp.pad(x, (0, pad)).reshape(n, -1)
    got = lax.all_to_all(parts, axis_names, 0, 0, tiled=False)
    mine = jnp.sum(got, axis=0) * scale
    back = lax.all_to_all(jnp.broadcast_to(mine[None], parts.shape), axis_names, 0, 0, tiled=False)
    return back.reshape(-1)[: x.shape[0]]


def slope_of(shifted, cotangent):
    sig = jax.nn.sigmoid(shifted)
    return (cotangent.astype(jnp.float32) * sig * (1.0 + shifted * (1.0 - sig))).astype(
        jnp.bfloat16
    )


def on_device(features, cotangent, weights, bias_term, adjacency, tile_rows, tile_cols, tile_count):
    tile_size = adjacency.shape[-1]
    slot_total = adjacency.shape[2]
    tile_data = adjacency.reshape(slot_total, tile_size, tile_size)
    row_ids = tile_rows.reshape(slot_total)
    col_ids = tile_cols.reshape(slot_total)
    in_count = tile_count.reshape(())
    n_row = lax.axis_size("row")
    n_col = lax.axis_size("col")
    own_rows = features.shape[0]
    own_blocks = own_rows // tile_size
    feat_width = features.shape[1]
    row_total = n_col * own_blocks
    col_total = n_row * own_blocks
    node_scale = 1.0 / math.sqrt(own_rows * n_row * n_col)

    me_col = lax.axis_index("col")
    rel_rows = relative_col(row_ids // own_blocks, me_col) * own_blocks + row_ids % own_blocks
    dense, dense_t = dense_blocks(tile_data, rel_rows, col_ids, in_count, row_total, col_total)

    projected = jnp.dot(features, weights, preferred_element_type=jnp.float32).astype(jnp.bfloat16)
    gathered = gather_by_a2a(projected, "row", n_row)
    partial_rows = jnp.dot(dense, gathered, preferred_element_type=jnp.float32)
    bias_row = bias_term[None, :]
    shifted = scatter_sum_col(partial_rows.reshape(n_col, own_rows, feat_width), n_col) + bias_row
    slope_own = slope_of(shifted, cotangent)
    slope_rows = gather_col(slope_own, n_col).reshape(n_col * own_rows, feat_width)
    activated = jax.nn.silu(shifted).astype(jnp.bfloat16)
    bias_part = jnp.sum(slope_own.astype(jnp.float32), axis=0)
    partial_cols = jnp.dot(dense_t, slope_rows, preferred_element_type=jnp.float32)
    back = scatter_sum_by_a2a(partial_cols, "row", n_row, jnp.bfloat16).astype(jnp.bfloat16)
    grad_input = lax.dot_general(
        back, weights, (((1,), (1,)), ((), ())), preferred_element_type=jnp.float32
    ).astype(jnp.bfloat16)
    weight_part = lax.dot_general(
        features, back, (((0,), (0,)), ((), ())), preferred_element_type=jnp.float32
    )
    joined = jnp.concatenate([weight_part.reshape(-1), bias_part])
    joined = all_sum_by_a2a(joined, ("row", "col"), n_row * n_col, node_scale)
    weight_sum = joined[: feat_width * feat_width].reshape(feat_width, feat_width)
    bias_sum = joined[feat_width * feat_width :]
    return (activated, grad_input, weight_sum, bias_sum)


def solution(mesh):
    return jax.shard_map(
        on_device,
        mesh=mesh,
        in_specs=(
            P(("row", "col"), None),
            P(("row", "col"), None),
            P(),
            P(),
            P("row", "col", None, None, None),
            P("row", "col", None),
            P("row", "col", None),
            P("row", "col"),
        ),
        out_specs=(P(("row", "col"), None), P(("row", "col"), None), P(), P()),
        check_vma=False,
    )
```

```python
import math

import jax
import jax.numpy as jnp
from jax import lax
from jax.experimental import pallas as pl
from jax.experimental.pallas import tpu as pltpu
from jax.sharding import PartitionSpec as P


def col_parts(c):
    return c // 4, (c // 2) % 2, c % 2


def relative_col(c2, me):
    y2, x2, k2 = col_parts(c2)
    y1, x1, k1 = col_parts(me)
    return ((y2 - y1) % 4) * 4 + (x2 ^ x1) * 2 + (k2 ^ k1)


def col_send(x, n, move):
    return lax.ppermute(x, "col", [(c, move(c)) for c in range(n)])


def y_up(c):
    return ((c // 4 + 1) % 4) * 4 + c % 4


def y_down(c):
    return ((c // 4 + 3) % 4) * 4 + c % 4


def scatter_sum_col(parts, n):
    rest = parts.shape[1:]
    parts = parts.reshape((4, 2, 2) + rest)
    acc = parts[:, :, 0] + col_send(parts[:, :, 1], n, lambda c: c ^ 1)
    via_up = col_send(acc[2, 0].astype(jnp.bfloat16), n, y_up).astype(jnp.float32)
    via_down = col_send(acc[2, 1].astype(jnp.bfloat16), n, y_down).astype(jnp.float32)
    to_up = jnp.stack([acc[1, 0] + via_up, acc[1, 1]]).astype(jnp.bfloat16)
    to_down = jnp.stack([acc[3, 0], acc[3, 1] + via_down]).astype(jnp.bfloat16)
    total = (
        acc[0]
        + col_send(to_up, n, y_up).astype(jnp.float32)
        + col_send(to_down, n, y_down).astype(jnp.float32)
    )
    return total[0] + col_send(total[1].astype(jnp.bfloat16), n, lambda c: c ^ 2).astype(jnp.float32)


def gather_col(own, n):
    pair = jnp.stack([own, col_send(own, n, lambda c: c ^ 2)])
    from_below = col_send(pair, n, y_up)
    from_above = col_send(pair, n, y_down)
    two_away = jnp.stack([col_send(from_above[0], n, y_down), col_send(from_below[1], n, y_up)])
    quad = jnp.stack([pair, from_above, two_away, from_below])
    full = jnp.stack([quad, col_send(quad, n, lambda c: c ^ 1)], axis=2)
    return full.reshape((16,) + own.shape)


def relative_row(r2, me):
    return ((r2 % 4 - me % 4) % 4) * 2 + ((r2 // 4) ^ (me // 4))


def row_send(x, n, move):
    return lax.ppermute(x, "row", [(r, move(r)) for r in range(n)])


def z_up(r):
    return (r // 4) * 4 + (r % 4 + 1) % 4


def z_down(r):
    return (r // 4) * 4 + (r % 4 + 3) % 4


def scatter_sum_row(parts, n):
    rest = parts.shape[1:]
    acc = parts.reshape((4, 2) + rest)
    via_up = row_send(acc[2, 0].astype(jnp.bfloat16), n, z_up).astype(jnp.float32)
    via_down = row_send(acc[2, 1].astype(jnp.bfloat16), n, z_down).astype(jnp.float32)
    to_up = jnp.stack([acc[1, 0] + via_up, acc[1, 1]]).astype(jnp.bfloat16)
    to_down = jnp.stack([acc[3, 0], acc[3, 1] + via_down]).astype(jnp.bfloat16)
    total = (
        acc[0]
        + row_send(to_up, n, z_up).astype(jnp.float32)
        + row_send(to_down, n, z_down).astype(jnp.float32)
    )
    return total[0] + row_send(total[1].astype(jnp.bfloat16), n, lambda r: r ^ 4).astype(jnp.float32)


def gather_row(own, n):
    pair = jnp.stack([own, row_send(own, n, lambda r: r ^ 4)])
    from_below = row_send(pair, n, z_up)
    from_above = row_send(pair, n, z_down)
    two_away = jnp.stack([row_send(from_above[0], n, z_down), row_send(from_below[1], n, z_up)])
    quad = jnp.stack([pair, from_above, two_away, from_below])
    return quad.reshape((8 * own.shape[0],) + own.shape[1:])


def place_kernel(slot_ref, adj_ref, dense_ref, dense_t_ref):
    row = pl.program_id(0)
    col_total = dense_ref.shape[1] // adj_ref.shape[-1]
    size = adj_ref.shape[-1]
    for col in range(col_total):
        slot = slot_ref[row * col_total + col]
        tile = adj_ref[jnp.maximum(slot, 0)]
        tile = jnp.where(slot >= 0, tile, jnp.zeros_like(tile))
        dense_ref[:, col * size : (col + 1) * size] = tile
        dense_t_ref[col * size : (col + 1) * size, :] = tile.T


def dense_blocks(tile_data, row_ids, col_ids, in_count, row_total, col_total):
    slot_total, size, _ = tile_data.shape
    slot_range = jnp.arange(slot_total, dtype=jnp.int32)
    pair_of = jnp.where(slot_range < in_count, row_ids * col_total + col_ids, -1)
    pair_range = jnp.arange(row_total * col_total, dtype=jnp.int32)
    slot_of = jnp.max(
        jnp.where(pair_range[:, None] == pair_of[None, :], slot_range[None, :], -1), axis=1
    )
    return pl.pallas_call(
        place_kernel,
        grid_spec=pltpu.PrefetchScalarGridSpec(
            num_scalar_prefetch=1,
            grid=(row_total,),
            in_specs=[pl.BlockSpec((slot_total, size, size), lambda r, slots: (0, 0, 0))],
            out_specs=[
                pl.BlockSpec((size, col_total * size), lambda r, slots: (r, 0)),
                pl.BlockSpec((col_total * size, size), lambda r, slots: (0, r)),
            ],
        ),
        out_shape=[
            jax.ShapeDtypeStruct((row_total * size, col_total * size), tile_data.dtype),
            jax.ShapeDtypeStruct((col_total * size, row_total * size), tile_data.dtype),
        ],
        compiler_params=pltpu.CompilerParams(vmem_limit_bytes=48 * 1024 * 1024),
        cost_estimate=pl.CostEstimate(
            flops=0,
            transcendentals=0,
            bytes_accessed=slot_total * size * size * 2 + 2 * row_total * col_total * size * size * 2,
        ),
    )(slot_of, tile_data)


def gather_by_a2a(x, axis_name, n):
    spread = jnp.broadcast_to(x[None], (n,) + x.shape)
    return lax.all_to_all(spread, axis_name, 0, 0, tiled=False).reshape((n * x.shape[0],) + x.shape[1:])


def scatter_sum_by_a2a(x, axis_name, n, link_dtype):
    parts = x.astype(link_dtype).reshape((n, x.shape[0] // n) + x.shape[1:])
    got = lax.all_to_all(parts, axis_name, 0, 0, tiled=False)
    return jnp.sum(got.astype(jnp.float32), axis=0)


def all_sum_by_a2a(x, axis_names, n, scale):
    pad = (-x.shape[0]) % n
    parts = jnp.pad(x, (0, pad)).reshape(n, -1)
    got = lax.all_to_all(parts, axis_names, 0, 0, tiled=False)
    mine = jnp.sum(got, axis=0) * scale
    back = lax.all_to_all(jnp.broadcast_to(mine[None], parts.shape), axis_names, 0, 0, tiled=False)
    return back.reshape(-1)[: x.shape[0]]


def slope_of(shifted, cotangent):
    sig = jax.nn.sigmoid(shifted)
    return (cotangent.astype(jnp.float32) * sig * (1.0 + shifted * (1.0 - sig))).astype(
        jnp.bfloat16
    )


def on_device(features, cotangent, weights, bias_term, adjacency, tile_rows, tile_cols, tile_count):
    tile_size = adjacency.shape[-1]
    slot_total = adjacency.shape[2]
    tile_data = adjacency.reshape(slot_total, tile_size, tile_size)
    row_ids = tile_rows.reshape(slot_total)
    col_ids = tile_cols.reshape(slot_total)
    in_count = tile_count.reshape(())
    n_row = lax.axis_size("row")
    n_col = lax.axis_size("col")
    own_rows = features.shape[0]
    own_blocks = own_rows // tile_size
    feat_width = features.shape[1]
    row_total = n_col * own_blocks
    col_total = n_row * own_blocks
    node_scale = 1.0 / math.sqrt(own_rows * n_row * n_col)

    me_col = lax.axis_index("col")
    rel_rows = relative_col(row_ids // own_blocks, me_col) * own_blocks + row_ids % own_blocks
    me_row = lax.axis_index("row")
    rel_cols = relative_row(col_ids // own_blocks, me_row) * own_blocks + col_ids % own_blocks
    dense, dense_t = dense_blocks(tile_data, rel_rows, rel_cols, in_count, row_total, col_total)

    projected = jnp.dot(features, weights, preferred_element_type=jnp.float32).astype(jnp.bfloat16)
    gathered = gather_row(projected, n_row)
    partial_rows = jnp.dot(dense, gathered, preferred_element_type=jnp.float32)
    bias_row = bias_term[None, :]
    shifted = scatter_sum_col(partial_rows.reshape(n_col, own_rows, feat_width), n_col) + bias_row
    slope_own = slope_of(shifted, cotangent)
    slope_rows = gather_col(slope_own, n_col).reshape(n_col * own_rows, feat_width)
    activated = jax.nn.silu(shifted).astype(jnp.bfloat16)
    bias_part = jnp.sum(slope_own.astype(jnp.float32), axis=0)
    partial_cols = jnp.dot(dense_t, slope_rows, preferred_element_type=jnp.float32)
    back = scatter_sum_row(partial_cols.reshape(n_row, own_rows, feat_width), n_row).astype(jnp.bfloat16)
    grad_input = lax.dot_general(
        back, weights, (((1,), (1,)), ((), ())), preferred_element_type=jnp.float32
    ).astype(jnp.bfloat16)
    weight_part = lax.dot_general(
        features, back, (((0,), (0,)), ((), ())), preferred_element_type=jnp.float32
    )
    joined = jnp.concatenate([weight_part.reshape(-1), bias_part])
    joined = all_sum_by_a2a(joined, ("row", "col"), n_row * n_col, node_scale)
    weight_sum = joined[: feat_width * feat_width].reshape(feat_width, feat_width)
    bias_sum = joined[feat_width * feat_width :]
    return (activated, grad_input, weight_sum, bias_sum)


def solution(mesh):
    return jax.shard_map(
        on_device,
        mesh=mesh,
        in_specs=(
            P(("row", "col"), None),
            P(("row", "col"), None),
            P(),
            P(),
            P("row", "col", None, None, None),
            P("row", "col", None),
            P("row", "col", None),
            P("row", "col"),
        ),
        out_specs=(P(("row", "col"), None), P(("row", "col"), None), P(), P()),
        check_vma=False,
    )
```

```python
import functools
import math

import jax
import jax.numpy as jnp
from jax import lax
from jax.experimental import pallas as pl
from jax.experimental.pallas import tpu as pltpu
from jax.sharding import PartitionSpec as P


def col_parts(c):
    return c // 4, (c // 2) % 2, c % 2


def relative_col(c2, me):
    y2, x2, k2 = col_parts(c2)
    y1, x1, k1 = col_parts(me)
    return ((y2 - y1) % 4) * 4 + (x2 ^ x1) * 2 + (k2 ^ k1)


def col_send(x, n, move):
    return lax.ppermute(x, "col", [(c, move(c)) for c in range(n)])


def y_up(c):
    return ((c // 4 + 1) % 4) * 4 + c % 4


def y_down(c):
    return ((c // 4 + 3) % 4) * 4 + c % 4


def scatter_sum_col(parts, n):
    rest = parts.shape[1:]
    parts = parts.reshape((4, 2, 2) + rest)
    acc = parts[:, :, 0] + col_send(parts[:, :, 1], n, lambda c: c ^ 1)
    via_up = col_send(acc[2, 0].astype(jnp.bfloat16), n, y_up).astype(jnp.float32)
    via_down = col_send(acc[2, 1].astype(jnp.bfloat16), n, y_down).astype(jnp.float32)
    to_up = jnp.stack([acc[1, 0] + via_up, acc[1, 1]]).astype(jnp.bfloat16)
    to_down = jnp.stack([acc[3, 0], acc[3, 1] + via_down]).astype(jnp.bfloat16)
    total = (
        acc[0]
        + col_send(to_up, n, y_up).astype(jnp.float32)
        + col_send(to_down, n, y_down).astype(jnp.float32)
    )
    return total[0] + col_send(total[1].astype(jnp.bfloat16), n, lambda c: c ^ 2).astype(jnp.float32)


def gather_col(own, n):
    pair = jnp.stack([own, col_send(own, n, lambda c: c ^ 2)])
    from_below = col_send(pair, n, y_up)
    from_above = col_send(pair, n, y_down)
    two_away = jnp.stack([col_send(from_above[0], n, y_down), col_send(from_below[1], n, y_up)])
    quad = jnp.stack([pair, from_above, two_away, from_below])
    full = jnp.stack([quad, col_send(quad, n, lambda c: c ^ 1)], axis=2)
    return full.reshape((16,) + own.shape)


def relative_row(r2, me):
    return ((r2 % 4 - me % 4) % 4) * 2 + ((r2 // 4) ^ (me // 4))


def row_send(x, n, move):
    return lax.ppermute(x, "row", [(r, move(r)) for r in range(n)])


def z_up(r):
    return (r // 4) * 4 + (r % 4 + 1) % 4


def z_down(r):
    return (r // 4) * 4 + (r % 4 + 3) % 4


def scatter_sum_row(parts, n):
    rest = parts.shape[1:]
    acc = parts.reshape((4, 2) + rest)
    via_up = row_send(acc[2, 0].astype(jnp.bfloat16), n, z_up).astype(jnp.float32)
    via_down = row_send(acc[2, 1].astype(jnp.bfloat16), n, z_down).astype(jnp.float32)
    to_up = jnp.stack([acc[1, 0] + via_up, acc[1, 1]]).astype(jnp.bfloat16)
    to_down = jnp.stack([acc[3, 0], acc[3, 1] + via_down]).astype(jnp.bfloat16)
    total = (
        acc[0]
        + row_send(to_up, n, z_up).astype(jnp.float32)
        + row_send(to_down, n, z_down).astype(jnp.float32)
    )
    return total[0] + row_send(total[1].astype(jnp.bfloat16), n, lambda r: r ^ 4).astype(jnp.float32)


def gather_row(own, n):
    pair = jnp.stack([own, row_send(own, n, lambda r: r ^ 4)])
    from_below = row_send(pair, n, z_up)
    from_above = row_send(pair, n, z_down)
    two_away = jnp.stack([row_send(from_above[0], n, z_down), row_send(from_below[1], n, z_up)])
    quad = jnp.stack([pair, from_above, two_away, from_below])
    return quad.reshape((8 * own.shape[0],) + own.shape[1:])


def place_kernel(row_offset, slot_ref, adj_ref, *refs):
    dense_ref, dense_t_ref = refs[-2], refs[-1]
    row = pl.program_id(0) + row_offset
    col_total = dense_ref.shape[1] // adj_ref.shape[-1]
    size = adj_ref.shape[-1]
    for col in range(col_total):
        slot = slot_ref[row * col_total + col]
        tile = adj_ref[jnp.maximum(slot, 0)]
        tile = jnp.where(slot >= 0, tile, jnp.zeros_like(tile))
        dense_ref[:, col * size : (col + 1) * size] = tile
        dense_t_ref[col * size : (col + 1) * size, :] = tile.T


def place_half(slot_of, tile_data, half, row_total, col_total, into=()):
    slot_total, size, _ = tile_data.shape
    rows_half = row_total // 2
    in_specs = [pl.BlockSpec((slot_total, size, size), lambda r, h, slots: (0, 0, 0))]
    in_specs += [pl.BlockSpec(memory_space=pl.ANY)] * len(into)
    return pl.pallas_call(
        functools.partial(place_kernel, half * rows_half),
        grid_spec=pltpu.PrefetchScalarGridSpec(
            num_scalar_prefetch=1,
            grid=(rows_half, 1),
            in_specs=in_specs,
            out_specs=[
                pl.BlockSpec((size, col_total * size), lambda r, h, slots: (r + half * rows_half, 0)),
                pl.BlockSpec((col_total * size, size), lambda r, h, slots: (0, r + half * rows_half)),
            ],
        ),
        out_shape=[
            jax.ShapeDtypeStruct((row_total * size, col_total * size), tile_data.dtype),
            jax.ShapeDtypeStruct((col_total * size, row_total * size), tile_data.dtype),
        ],
        input_output_aliases={2: 0, 3: 1} if into else {},
        compiler_params=pltpu.CompilerParams(vmem_limit_bytes=48 * 1024 * 1024),
        cost_estimate=pl.CostEstimate(
            flops=0,
            transcendentals=0,
            bytes_accessed=slot_total * size * size * 2 + row_total * col_total * size * size * 2,
        ),
    )(slot_of, tile_data, *into)


def slot_table(row_ids, col_ids, in_count, slot_total, row_total, col_total):
    slot_range = jnp.arange(slot_total, dtype=jnp.int32)
    pair_of = jnp.where(slot_range < in_count, row_ids * col_total + col_ids, -1)
    pair_range = jnp.arange(row_total * col_total, dtype=jnp.int32)
    return jnp.max(
        jnp.where(pair_range[:, None] == pair_of[None, :], slot_range[None, :], -1), axis=1
    )


def all_sum_by_a2a(x, axis_names, n, scale):
    pad = (-x.shape[0]) % n
    parts = jnp.pad(x, (0, pad)).reshape(n, -1)
    got = lax.all_to_all(parts, axis_names, 0, 0, tiled=False)
    mine = jnp.sum(got, axis=0) * scale
    back = lax.all_to_all(jnp.broadcast_to(mine[None], parts.shape), axis_names, 0, 0, tiled=False)
    return back.reshape(-1)[: x.shape[0]]


def slope_of(shifted, cotangent):
    sig = jax.nn.sigmoid(shifted)
    return (cotangent.astype(jnp.float32) * sig * (1.0 + shifted * (1.0 - sig))).astype(
        jnp.bfloat16
    )


def on_device_body(features, cotangent, weights, bias_term, adjacency, tile_rows, tile_cols, tile_count):
    tile_size = adjacency.shape[-1]
    slot_total = adjacency.shape[2]
    tile_data = adjacency.reshape(slot_total, tile_size, tile_size)
    row_ids = tile_rows.reshape(slot_total)
    col_ids = tile_cols.reshape(slot_total)
    in_count = tile_count.reshape(())
    n_row = lax.axis_size("row")
    n_col = lax.axis_size("col")
    own_rows = features.shape[0]
    own_blocks = own_rows // tile_size
    feat_width = features.shape[1]
    row_total = n_col * own_blocks
    col_total = n_row * own_blocks
    node_scale = 1.0 / math.sqrt(own_rows * n_row * n_col)

    me_col = lax.axis_index("col")
    rel_rows = relative_col(row_ids // own_blocks, me_col) * own_blocks + row_ids % own_blocks
    me_row = lax.axis_index("row")
    rel_cols = relative_row(col_ids // own_blocks, me_row) * own_blocks + col_ids % own_blocks
    slot_of = slot_table(rel_rows, rel_cols, in_count, slot_total, row_total, col_total)
    first = place_half(slot_of, tile_data, 0, row_total, col_total)
    dense, dense_t = place_half(slot_of, tile_data, 1, row_total, col_total, tuple(first))

    projected = jnp.dot(features, weights, preferred_element_type=jnp.float32).astype(jnp.bfloat16)
    gathered = gather_row(projected, n_row)
    partial_rows = jnp.dot(dense, gathered, preferred_element_type=jnp.float32)
    bias_row = bias_term[None, :]
    shifted = scatter_sum_col(partial_rows.reshape(n_col, own_rows, feat_width), n_col) + bias_row
    slope_own = slope_of(shifted, cotangent)
    slope_rows = gather_col(slope_own, n_col).reshape(n_col * own_rows, feat_width)
    activated = jax.nn.silu(shifted).astype(jnp.bfloat16)
    bias_part = jnp.sum(slope_own.astype(jnp.float32), axis=0)
    partial_cols = jnp.dot(dense_t, slope_rows, preferred_element_type=jnp.float32)
    back = scatter_sum_row(partial_cols.reshape(n_row, own_rows, feat_width), n_row).astype(jnp.bfloat16)
    grad_input = lax.dot_general(
        back, weights, (((1,), (1,)), ((), ())), preferred_element_type=jnp.float32
    ).astype(jnp.bfloat16)
    weight_part = lax.dot_general(
        features, back, (((0,), (0,)), ((), ())), preferred_element_type=jnp.float32
    )
    joined = jnp.concatenate([weight_part.reshape(-1), bias_part])
    joined = all_sum_by_a2a(joined, ("row", "col"), n_row * n_col, node_scale)
    weight_sum = joined[: feat_width * feat_width].reshape(feat_width, feat_width)
    bias_sum = joined[feat_width * feat_width :]
    return (activated, grad_input, weight_sum, bias_sum)


def solution(mesh):
    return sharded(mesh)


def sharded(mesh):
    return jax.shard_map(
        on_device_body,
        mesh=mesh,
        in_specs=(
            P(("row", "col"), None),
            P(("row", "col"), None),
            P(),
            P(),
            P("row", "col", None, None, None),
            P("row", "col", None),
            P("row", "col", None),
            P("row", "col"),
        ),
        out_specs=(P(("row", "col"), None), P(("row", "col"), None), P(), P()),
        check_vma=False,
    )
```

```python
import math

import jax
import jax.numpy as jnp
from jax import lax
from jax.experimental import pallas as pl
from jax.experimental.pallas import tpu as pltpu
from jax.sharding import PartitionSpec as P


def col_parts(c):
    return c // 4, (c // 2) % 2, c % 2


def relative_col(c2, me):
    y2, x2, k2 = col_parts(c2)
    y1, x1, k1 = col_parts(me)
    return (k2 ^ k1) * 8 + ((y2 - y1) % 4) * 2 + (x2 ^ x1)


def col_send(x, n, move):
    return lax.ppermute(x, "col", [(c, move(c)) for c in range(n)])


def y_up(c):
    return ((c // 4 + 1) % 4) * 4 + c % 4


def y_down(c):
    return ((c // 4 + 3) % 4) * 4 + c % 4


def scatter_sum_col(mine, other, n):
    rest = mine.shape[1:]
    got = col_send(other.reshape((4, 2) + rest), n, lambda c: c ^ 1)
    acc = mine.reshape((4, 2) + rest) + got
    via_up = col_send(acc[2, 0].astype(jnp.bfloat16), n, y_up).astype(jnp.float32)
    via_down = col_send(acc[2, 1].astype(jnp.bfloat16), n, y_down).astype(jnp.float32)
    to_up = jnp.stack([acc[1, 0] + via_up, acc[1, 1]]).astype(jnp.bfloat16)
    to_down = jnp.stack([acc[3, 0], acc[3, 1] + via_down]).astype(jnp.bfloat16)
    total = (
        acc[0]
        + col_send(to_up, n, y_up).astype(jnp.float32)
        + col_send(to_down, n, y_down).astype(jnp.float32)
    )
    return total[0] + col_send(total[1].astype(jnp.bfloat16), n, lambda c: c ^ 2).astype(jnp.float32)


def gather_col(own, n):
    pair = jnp.stack([own, col_send(own, n, lambda c: c ^ 2)])
    from_below = col_send(pair, n, y_up)
    from_above = col_send(pair, n, y_down)
    two_away = jnp.stack([col_send(from_above[0], n, y_down), col_send(from_below[1], n, y_up)])
    quad = jnp.stack([pair, from_above, two_away, from_below])
    rows = (8 * own.shape[0],) + own.shape[1:]
    return quad.reshape(rows), col_send(quad, n, lambda c: c ^ 1).reshape(rows)


def place_kernel(slot_ref, adj_ref, dense_ref, dense_t_ref):
    row = pl.program_id(0)
    col_total = dense_ref.shape[1] // adj_ref.shape[-1]
    size = adj_ref.shape[-1]
    for col in range(col_total):
        slot = slot_ref[row * col_total + col]
        tile = adj_ref[jnp.maximum(slot, 0)]
        tile = jnp.where(slot >= 0, tile, jnp.zeros_like(tile))
        dense_ref[:, col * size : (col + 1) * size] = tile
        dense_t_ref[col * size : (col + 1) * size, :] = tile.T


def dense_blocks(tile_data, row_ids, col_ids, in_count, row_total, col_total):
    slot_total, size, _ = tile_data.shape
    slot_range = jnp.arange(slot_total, dtype=jnp.int32)
    pair_of = jnp.where(slot_range < in_count, row_ids * col_total + col_ids, -1)
    pair_range = jnp.arange(row_total * col_total, dtype=jnp.int32)
    slot_of = jnp.max(
        jnp.where(pair_range[:, None] == pair_of[None, :], slot_range[None, :], -1), axis=1
    )
    return pl.pallas_call(
        place_kernel,
        grid_spec=pltpu.PrefetchScalarGridSpec(
            num_scalar_prefetch=1,
            grid=(row_total,),
            in_specs=[pl.BlockSpec((slot_total, size, size), lambda r, slots: (0, 0, 0))],
            out_specs=[
                pl.BlockSpec((size, col_total * size), lambda r, slots: (r, 0)),
                pl.BlockSpec(
                    (None, col_total * size, size),
                    lambda r, slots: (r // (row_total // 2), 0, r % (row_total // 2)),
                ),
            ],
        ),
        out_shape=[
            jax.ShapeDtypeStruct((row_total * size, col_total * size), tile_data.dtype),
            jax.ShapeDtypeStruct((2, col_total * size, row_total * size // 2), tile_data.dtype),
        ],
        compiler_params=pltpu.CompilerParams(vmem_limit_bytes=48 * 1024 * 1024),
        cost_estimate=pl.CostEstimate(
            flops=0,
            transcendentals=0,
            bytes_accessed=slot_total * size * size * 2 + 2 * row_total * col_total * size * size * 2,
        ),
    )(slot_of, tile_data)


def gather_by_a2a(x, axis_name, n):
    spread = jnp.broadcast_to(x[None], (n,) + x.shape)
    return lax.all_to_all(spread, axis_name, 0, 0, tiled=False).reshape((n * x.shape[0],) + x.shape[1:])


def scatter_sum_by_a2a(x, axis_name, n, link_dtype):
    parts = x.astype(link_dtype).reshape((n, x.shape[0] // n) + x.shape[1:])
    got = lax.all_to_all(parts, axis_name, 0, 0, tiled=False)
    return jnp.sum(got.astype(jnp.float32), axis=0)


def all_sum_by_a2a(x, axis_names, n, scale):
    pad = (-x.shape[0]) % n
    parts = jnp.pad(x, (0, pad)).reshape(n, -1)
    got = lax.all_to_all(parts, axis_names, 0, 0, tiled=False)
    mine = jnp.sum(got, axis=0) * scale
    back = lax.all_to_all(jnp.broadcast_to(mine[None], parts.shape), axis_names, 0, 0, tiled=False)
    return back.reshape(-1)[: x.shape[0]]


def slope_of(shifted, cotangent):
    sig = jax.nn.sigmoid(shifted)
    return (cotangent.astype(jnp.float32) * sig * (1.0 + shifted * (1.0 - sig))).astype(
        jnp.bfloat16
    )


def on_device(features, cotangent, weights, bias_term, adjacency, tile_rows, tile_cols, tile_count):
    tile_size = adjacency.shape[-1]
    slot_total = adjacency.shape[2]
    tile_data = adjacency.reshape(slot_total, tile_size, tile_size)
    row_ids = tile_rows.reshape(slot_total)
    col_ids = tile_cols.reshape(slot_total)
    in_count = tile_count.reshape(())
    n_row = lax.axis_size("row")
    n_col = lax.axis_size("col")
    own_rows = features.shape[0]
    own_blocks = own_rows // tile_size
    feat_width = features.shape[1]
    row_total = n_col * own_blocks
    col_total = n_row * own_blocks
    node_scale = 1.0 / math.sqrt(own_rows * n_row * n_col)

    me_col = lax.axis_index("col")
    rel_rows = relative_col(row_ids // own_blocks, me_col) * own_blocks + row_ids % own_blocks
    dense, dense_t = dense_blocks(tile_data, rel_rows, col_ids, in_count, row_total, col_total)

    projected = jnp.dot(features, weights, preferred_element_type=jnp.float32).astype(jnp.bfloat16)
    gathered = gather_by_a2a(projected, "row", n_row)
    half = row_total * tile_size // 2
    other_rows = jnp.dot(dense[half:], gathered, preferred_element_type=jnp.float32)
    mine_rows = lax.optimization_barrier(
        jnp.dot(dense[:half], gathered, preferred_element_type=jnp.float32)
    )
    bias_row = bias_term[None, :]
    shifted = (
        scatter_sum_col(
            mine_rows.reshape(n_col // 2, own_rows, feat_width),
            other_rows.reshape(n_col // 2, own_rows, feat_width),
            n_col,
        )
        + bias_row
    )
    slope_own = slope_of(shifted, cotangent)
    slope_mine, slope_other = gather_col(slope_own, n_col)
    activated = jax.nn.silu(shifted).astype(jnp.bfloat16)
    bias_part = jnp.sum(slope_own.astype(jnp.float32), axis=0)
    cols_mine = lax.optimization_barrier(
        jnp.dot(dense_t[0], slope_mine, preferred_element_type=jnp.float32)
    )
    partial_cols = cols_mine + jnp.dot(dense_t[1], slope_other, preferred_element_type=jnp.float32)
    back = scatter_sum_by_a2a(partial_cols, "row", n_row, jnp.bfloat16).astype(jnp.bfloat16)
    grad_input = lax.dot_general(
        back, weights, (((1,), (1,)), ((), ())), preferred_element_type=jnp.float32
    ).astype(jnp.bfloat16)
    weight_part = lax.dot_general(
        features, back, (((0,), (0,)), ((), ())), preferred_element_type=jnp.float32
    )
    joined = jnp.concatenate([weight_part.reshape(-1), bias_part])
    joined = all_sum_by_a2a(joined, ("row", "col"), n_row * n_col, node_scale)
    weight_sum = joined[: feat_width * feat_width].reshape(feat_width, feat_width)
    bias_sum = joined[feat_width * feat_width :]
    return (activated, grad_input, weight_sum, bias_sum)


def solution(mesh):
    return jax.shard_map(
        on_device,
        mesh=mesh,
        in_specs=(
            P(("row", "col"), None),
            P(("row", "col"), None),
            P(),
            P(),
            P("row", "col", None, None, None),
            P("row", "col", None),
            P("row", "col", None),
            P("row", "col"),
        ),
        out_specs=(P(("row", "col"), None), P(("row", "col"), None), P(), P()),
        check_vma=False,
    )
```

```python
import math

import jax
import jax.numpy as jnp
from jax import lax
from jax.experimental import pallas as pl
from jax.experimental.pallas import tpu as pltpu
from jax.sharding import PartitionSpec as P


def col_parts(c):
    return c // 4, (c // 2) % 2, c % 2


def relative_col(c2, me):
    y2, x2, k2 = col_parts(c2)
    y1, x1, k1 = col_parts(me)
    return (k2 ^ k1) * 8 + ((y2 - y1) % 4) * 2 + (x2 ^ x1)


def col_send(x, n, move):
    return lax.ppermute(x, "col", [(c, move(c)) for c in range(n)])


def y_up(c):
    return ((c // 4 + 1) % 4) * 4 + c % 4


def y_down(c):
    return ((c // 4 + 3) % 4) * 4 + c % 4


def scatter_sum_col(mine, other, n):
    rest = mine.shape[1:]
    got = col_send(other.reshape((4, 2) + rest), n, lambda c: c ^ 1)
    acc = mine.reshape((4, 2) + rest) + got
    via_up = col_send(acc[2, 0].astype(jnp.bfloat16), n, y_up).astype(jnp.float32)
    via_down = col_send(acc[2, 1].astype(jnp.bfloat16), n, y_down).astype(jnp.float32)
    to_up = jnp.stack([acc[1, 0] + via_up, acc[1, 1]]).astype(jnp.bfloat16)
    to_down = jnp.stack([acc[3, 0], acc[3, 1] + via_down]).astype(jnp.bfloat16)
    total = (
        acc[0]
        + col_send(to_up, n, y_up).astype(jnp.float32)
        + col_send(to_down, n, y_down).astype(jnp.float32)
    )
    return total[0] + col_send(total[1].astype(jnp.bfloat16), n, lambda c: c ^ 2).astype(jnp.float32)


def gather_col(own, n):
    pair = jnp.stack([own, col_send(own, n, lambda c: c ^ 2)])
    from_below = col_send(pair, n, y_up)
    from_above = col_send(pair, n, y_down)
    two_away = jnp.stack([col_send(from_above[0], n, y_down), col_send(from_below[1], n, y_up)])
    quad = jnp.stack([pair, from_above, two_away, from_below])
    rows = (8 * own.shape[0],) + own.shape[1:]
    return quad.reshape(rows), col_send(quad, n, lambda c: c ^ 1).reshape(rows)


def place_kernel(slot_ref, adj_ref, mine_ref, other_ref, dense_t_ref):
    half = pl.program_id(0)
    row = half * pl.num_programs(1) + pl.program_id(1)
    col_total = mine_ref.shape[1] // adj_ref.shape[-1]
    size = adj_ref.shape[-1]
    for col in range(col_total):
        slot = slot_ref[row * col_total + col]
        tile = adj_ref[jnp.maximum(slot, 0)]
        tile = jnp.where(slot >= 0, tile, jnp.zeros_like(tile))

        @pl.when(half == 0)
        def _():
            mine_ref[:, col * size : (col + 1) * size] = tile

        @pl.when(half == 1)
        def _():
            other_ref[:, col * size : (col + 1) * size] = tile

        dense_t_ref[col * size : (col + 1) * size, :] = tile.T


def dense_blocks(tile_data, row_ids, col_ids, in_count, row_total, col_total):
    slot_total, size, _ = tile_data.shape
    slot_range = jnp.arange(slot_total, dtype=jnp.int32)
    pair_of = jnp.where(slot_range < in_count, row_ids * col_total + col_ids, -1)
    pair_range = jnp.arange(row_total * col_total, dtype=jnp.int32)
    slot_of = jnp.max(
        jnp.where(pair_range[:, None] == pair_of[None, :], slot_range[None, :], -1), axis=1
    )
    return pl.pallas_call(
        place_kernel,
        grid_spec=pltpu.PrefetchScalarGridSpec(
            num_scalar_prefetch=1,
            grid=(2, row_total // 2),
            in_specs=[pl.BlockSpec((slot_total, size, size), lambda h, r, slots: (0, 0, 0))],
            out_specs=[
                pl.BlockSpec(
                    (size, col_total * size),
                    lambda h, r, slots: (jnp.where(h == 0, r, row_total // 2 - 1), 0),
                ),
                pl.BlockSpec(
                    (size, col_total * size), lambda h, r, slots: (jnp.where(h == 1, r, 0), 0)
                ),
                pl.BlockSpec((None, col_total * size, size), lambda h, r, slots: (h, 0, r)),
            ],
        ),
        out_shape=[
            jax.ShapeDtypeStruct((row_total * size // 2, col_total * size), tile_data.dtype),
            jax.ShapeDtypeStruct((row_total * size // 2, col_total * size), tile_data.dtype),
            jax.ShapeDtypeStruct((2, col_total * size, row_total * size // 2), tile_data.dtype),
        ],
        compiler_params=pltpu.CompilerParams(vmem_limit_bytes=48 * 1024 * 1024),
        cost_estimate=pl.CostEstimate(
            flops=0,
            transcendentals=0,
            bytes_accessed=slot_total * size * size * 2 + 2 * row_total * col_total * size * size * 2,
        ),
    )(slot_of, tile_data)


def gather_by_a2a(x, axis_name, n):
    spread = jnp.broadcast_to(x[None], (n,) + x.shape)
    return lax.all_to_all(spread, axis_name, 0, 0, tiled=False).reshape((n * x.shape[0],) + x.shape[1:])


def scatter_sum_by_a2a(x, axis_name, n, link_dtype):
    parts = x.astype(link_dtype).reshape((n, x.shape[0] // n) + x.shape[1:])
    got = lax.all_to_all(parts, axis_name, 0, 0, tiled=False)
    return jnp.sum(got.astype(jnp.float32), axis=0)


def all_sum_by_a2a(x, axis_names, n, scale):
    pad = (-x.shape[0]) % n
    parts = jnp.pad(x, (0, pad)).reshape(n, -1)
    got = lax.all_to_all(parts, axis_names, 0, 0, tiled=False)
    mine = jnp.sum(got, axis=0) * scale
    back = lax.all_to_all(jnp.broadcast_to(mine[None], parts.shape), axis_names, 0, 0, tiled=False)
    return back.reshape(-1)[: x.shape[0]]


def slope_of(shifted, cotangent):
    sig = jax.nn.sigmoid(shifted)
    return (cotangent.astype(jnp.float32) * sig * (1.0 + shifted * (1.0 - sig))).astype(
        jnp.bfloat16
    )


def on_device(features, cotangent, weights, bias_term, adjacency, tile_rows, tile_cols, tile_count):
    tile_size = adjacency.shape[-1]
    slot_total = adjacency.shape[2]
    tile_data = adjacency.reshape(slot_total, tile_size, tile_size)
    row_ids = tile_rows.reshape(slot_total)
    col_ids = tile_cols.reshape(slot_total)
    in_count = tile_count.reshape(())
    n_row = lax.axis_size("row")
    n_col = lax.axis_size("col")
    own_rows = features.shape[0]
    own_blocks = own_rows // tile_size
    feat_width = features.shape[1]
    row_total = n_col * own_blocks
    col_total = n_row * own_blocks
    node_scale = 1.0 / math.sqrt(own_rows * n_row * n_col)

    me_col = lax.axis_index("col")
    rel_rows = relative_col(row_ids // own_blocks, me_col) * own_blocks + row_ids % own_blocks
    dense_mine, dense_other, dense_t = dense_blocks(tile_data, rel_rows, col_ids, in_count, row_total, col_total)

    projected = jnp.dot(features, weights, preferred_element_type=jnp.float32).astype(jnp.bfloat16)
    gathered = gather_by_a2a(projected, "row", n_row)
    other_rows = jnp.dot(dense_other, gathered, preferred_element_type=jnp.float32)
    mine_rows = lax.optimization_barrier(
        jnp.dot(dense_mine, gathered, preferred_element_type=jnp.float32)
    )
    bias_row = bias_term[None, :]
    shifted = (
        scatter_sum_col(
            mine_rows.reshape(n_col // 2, own_rows, feat_width),
            other_rows.reshape(n_col // 2, own_rows, feat_width),
            n_col,
        )
        + bias_row
    )
    slope_own = slope_of(shifted, cotangent)
    slope_mine, slope_other = gather_col(slope_own, n_col)
    activated = jax.nn.silu(shifted).astype(jnp.bfloat16)
    bias_part = jnp.sum(slope_own.astype(jnp.float32), axis=0)
    cols_mine = lax.optimization_barrier(
        jnp.dot(dense_t[0], slope_mine, preferred_element_type=jnp.float32)
    )
    partial_cols = cols_mine + jnp.dot(dense_t[1], slope_other, preferred_element_type=jnp.float32)
    back = scatter_sum_by_a2a(partial_cols, "row", n_row, jnp.bfloat16).astype(jnp.bfloat16)
    grad_input = lax.dot_general(
        back, weights, (((1,), (1,)), ((), ())), preferred_element_type=jnp.float32
    ).astype(jnp.bfloat16)
    weight_part = lax.dot_general(
        features, back, (((0,), (0,)), ((), ())), preferred_element_type=jnp.float32
    )
    joined = jnp.concatenate([weight_part.reshape(-1), bias_part])
    joined = all_sum_by_a2a(joined, ("row", "col"), n_row * n_col, node_scale)
    weight_sum = joined[: feat_width * feat_width].reshape(feat_width, feat_width)
    bias_sum = joined[feat_width * feat_width :]
    return (activated, grad_input, weight_sum, bias_sum)


def solution(mesh):
    return jax.shard_map(
        on_device,
        mesh=mesh,
        in_specs=(
            P(("row", "col"), None),
            P(("row", "col"), None),
            P(),
            P(),
            P("row", "col", None, None, None),
            P("row", "col", None),
            P("row", "col", None),
            P("row", "col"),
        ),
        out_specs=(P(("row", "col"), None), P(("row", "col"), None), P(), P()),
        check_vma=False,
    )
```

```python
import functools
import math

import jax
import jax.numpy as jnp
from jax import lax
from jax.experimental import pallas as pl
from jax.experimental.pallas import tpu as pltpu
from jax.sharding import PartitionSpec as P


def col_parts(c):
    return c // 4, (c // 2) % 2, c % 2


def relative_col(c2, me):
    y2, x2, k2 = col_parts(c2)
    y1, x1, k1 = col_parts(me)
    return (k2 ^ k1) * 8 + ((y2 - y1) % 4) * 2 + (x2 ^ x1)


def col_send(x, n, move):
    return lax.ppermute(x, "col", [(c, move(c)) for c in range(n)])


def y_up(c):
    return ((c // 4 + 1) % 4) * 4 + c % 4


def y_down(c):
    return ((c // 4 + 3) % 4) * 4 + c % 4


def scatter_sum_col(mine, other, n):
    rest = mine.shape[1:]
    got = col_send(other.reshape((4, 2) + rest), n, lambda c: c ^ 1)
    acc = mine.reshape((4, 2) + rest) + got
    via_up = col_send(acc[2, 0].astype(jnp.bfloat16), n, y_up).astype(jnp.float32)
    via_down = col_send(acc[2, 1].astype(jnp.bfloat16), n, y_down).astype(jnp.float32)
    to_up = jnp.stack([acc[1, 0] + via_up, acc[1, 1]]).astype(jnp.bfloat16)
    to_down = jnp.stack([acc[3, 0], acc[3, 1] + via_down]).astype(jnp.bfloat16)
    total = (
        acc[0]
        + col_send(to_up, n, y_up).astype(jnp.float32)
        + col_send(to_down, n, y_down).astype(jnp.float32)
    )
    return total[0] + col_send(total[1].astype(jnp.bfloat16), n, lambda c: c ^ 2).astype(jnp.float32)


def gather_col(own, n):
    pair = jnp.stack([own, col_send(own, n, lambda c: c ^ 2)])
    from_below = col_send(pair, n, y_up)
    from_above = col_send(pair, n, y_down)
    two_away = jnp.stack([col_send(from_above[0], n, y_down), col_send(from_below[1], n, y_up)])
    quad = jnp.stack([pair, from_above, two_away, from_below])
    rows = (8 * own.shape[0],) + own.shape[1:]
    return quad.reshape(rows), col_send(quad, n, lambda c: c ^ 1).reshape(rows)


def place_kernel(row_offset, slot_ref, adj_ref, dense_ref, dense_t_ref):
    row = pl.program_id(0) + row_offset
    col_total = dense_ref.shape[1] // adj_ref.shape[-1]
    size = adj_ref.shape[-1]
    for col in range(col_total):
        slot = slot_ref[row * col_total + col]
        tile = adj_ref[jnp.maximum(slot, 0)]
        tile = jnp.where(slot >= 0, tile, jnp.zeros_like(tile))
        dense_ref[:, col * size : (col + 1) * size] = tile
        dense_t_ref[col * size : (col + 1) * size, :] = tile.T


def place_rows(slot_of, tile_data, row_offset, row_count, col_total):
    slot_total, size, _ = tile_data.shape
    return pl.pallas_call(
        functools.partial(place_kernel, row_offset),
        grid_spec=pltpu.PrefetchScalarGridSpec(
            num_scalar_prefetch=1,
            grid=(row_count,),
            in_specs=[pl.BlockSpec((slot_total, size, size), lambda r, slots: (0, 0, 0))],
            out_specs=[
                pl.BlockSpec((size, col_total * size), lambda r, slots: (r, 0)),
                pl.BlockSpec((col_total * size, size), lambda r, slots: (0, r)),
            ],
        ),
        out_shape=[
            jax.ShapeDtypeStruct((row_count * size, col_total * size), tile_data.dtype),
            jax.ShapeDtypeStruct((col_total * size, row_count * size), tile_data.dtype),
        ],
        compiler_params=pltpu.CompilerParams(vmem_limit_bytes=48 * 1024 * 1024),
        cost_estimate=pl.CostEstimate(
            flops=0,
            transcendentals=0,
            bytes_accessed=slot_total * size * size * 2 + 2 * row_count * col_total * size * size * 2,
        ),
    )(slot_of, tile_data)


def dense_blocks(tile_data, row_ids, col_ids, in_count, row_total, col_total):
    slot_total = tile_data.shape[0]
    slot_range = jnp.arange(slot_total, dtype=jnp.int32)
    pair_of = jnp.where(slot_range < in_count, row_ids * col_total + col_ids, -1)
    pair_range = jnp.arange(row_total * col_total, dtype=jnp.int32)
    slot_of = jnp.max(
        jnp.where(pair_range[:, None] == pair_of[None, :], slot_range[None, :], -1), axis=1
    )
    half = row_total // 2
    mine, mine_t = place_rows(slot_of, tile_data, 0, half, col_total)
    other, other_t = place_rows(slot_of, tile_data, half, half, col_total)
    return mine, other, mine_t, other_t


def gather_by_a2a(x, axis_name, n):
    spread = jnp.broadcast_to(x[None], (n,) + x.shape)
    return lax.all_to_all(spread, axis_name, 0, 0, tiled=False).reshape((n * x.shape[0],) + x.shape[1:])


def scatter_sum_by_a2a(x, axis_name, n, link_dtype):
    parts = x.astype(link_dtype).reshape((n, x.shape[0] // n) + x.shape[1:])
    got = lax.all_to_all(parts, axis_name, 0, 0, tiled=False)
    return jnp.sum(got.astype(jnp.float32), axis=0)


def all_sum_by_a2a(x, axis_names, n, scale):
    pad = (-x.shape[0]) % n
    parts = jnp.pad(x, (0, pad)).reshape(n, -1)
    got = lax.all_to_all(parts, axis_names, 0, 0, tiled=False)
    mine = jnp.sum(got, axis=0) * scale
    back = lax.all_to_all(jnp.broadcast_to(mine[None], parts.shape), axis_names, 0, 0, tiled=False)
    return back.reshape(-1)[: x.shape[0]]


def slope_of(shifted, cotangent):
    sig = jax.nn.sigmoid(shifted)
    return (cotangent.astype(jnp.float32) * sig * (1.0 + shifted * (1.0 - sig))).astype(
        jnp.bfloat16
    )


def on_device(features, cotangent, weights, bias_term, adjacency, tile_rows, tile_cols, tile_count):
    tile_size = adjacency.shape[-1]
    slot_total = adjacency.shape[2]
    tile_data = adjacency.reshape(slot_total, tile_size, tile_size)
    row_ids = tile_rows.reshape(slot_total)
    col_ids = tile_cols.reshape(slot_total)
    in_count = tile_count.reshape(())
    n_row = lax.axis_size("row")
    n_col = lax.axis_size("col")
    own_rows = features.shape[0]
    own_blocks = own_rows // tile_size
    feat_width = features.shape[1]
    row_total = n_col * own_blocks
    col_total = n_row * own_blocks
    node_scale = 1.0 / math.sqrt(own_rows * n_row * n_col)

    me_col = lax.axis_index("col")
    rel_rows = relative_col(row_ids // own_blocks, me_col) * own_blocks + row_ids % own_blocks
    dense_mine, dense_other, dense_t_mine, dense_t_other = dense_blocks(tile_data, rel_rows, col_ids, in_count, row_total, col_total)

    projected = jnp.dot(features, weights, preferred_element_type=jnp.float32).astype(jnp.bfloat16)
    gathered = gather_by_a2a(projected, "row", n_row)
    other_rows = jnp.dot(dense_other, gathered, preferred_element_type=jnp.float32)
    mine_rows = lax.optimization_barrier(
        jnp.dot(dense_mine, gathered, preferred_element_type=jnp.float32)
    )
    bias_row = bias_term[None, :]
    shifted = (
        scatter_sum_col(
            mine_rows.reshape(n_col // 2, own_rows, feat_width),
            other_rows.reshape(n_col // 2, own_rows, feat_width),
            n_col,
        )
        + bias_row
    )
    slope_own = slope_of(shifted, cotangent)
    slope_mine, slope_other = gather_col(slope_own, n_col)
    activated = jax.nn.silu(shifted).astype(jnp.bfloat16)
    bias_part = jnp.sum(slope_own.astype(jnp.float32), axis=0)
    cols_mine = lax.optimization_barrier(
        jnp.dot(dense_t_mine, slope_mine, preferred_element_type=jnp.float32)
    )
    partial_cols = cols_mine + jnp.dot(dense_t_other, slope_other, preferred_element_type=jnp.float32)
    back = scatter_sum_by_a2a(partial_cols, "row", n_row, jnp.bfloat16).astype(jnp.bfloat16)
    grad_input = lax.dot_general(
        back, weights, (((1,), (1,)), ((), ())), preferred_element_type=jnp.float32
    ).astype(jnp.bfloat16)
    weight_part = lax.dot_general(
        features, back, (((0,), (0,)), ((), ())), preferred_element_type=jnp.float32
    )
    joined = jnp.concatenate([weight_part.reshape(-1), bias_part])
    joined = all_sum_by_a2a(joined, ("row", "col"), n_row * n_col, node_scale)
    weight_sum = joined[: feat_width * feat_width].reshape(feat_width, feat_width)
    bias_sum = joined[feat_width * feat_width :]
    return (activated, grad_input, weight_sum, bias_sum)


def solution(mesh):
    return jax.shard_map(
        on_device,
        mesh=mesh,
        in_specs=(
            P(("row", "col"), None),
            P(("row", "col"), None),
            P(),
            P(),
            P("row", "col", None, None, None),
            P("row", "col", None),
            P("row", "col", None),
            P("row", "col"),
        ),
        out_specs=(P(("row", "col"), None), P(("row", "col"), None), P(), P()),
        check_vma=False,
    )
```

```python
import functools
import math

import jax
import jax.numpy as jnp
from jax import lax
from jax.experimental import pallas as pl
from jax.experimental.pallas import tpu as pltpu
from jax.sharding import PartitionSpec as P


def col_parts(c):
    return c // 4, (c // 2) % 2, c % 2


def relative_col(c2, me):
    y2, x2, k2 = col_parts(c2)
    y1, x1, k1 = col_parts(me)
    return (k2 ^ k1) * 8 + ((y2 - y1) % 4) * 2 + (x2 ^ x1)


def col_send(x, n, move):
    return lax.ppermute(x, "col", [(c, move(c)) for c in range(n)])


def y_up(c):
    return ((c // 4 + 1) % 4) * 4 + c % 4


def y_down(c):
    return ((c // 4 + 3) % 4) * 4 + c % 4


def scatter_sum_col(mine, other, n):
    rest = mine.shape[1:]
    got = col_send(other.reshape((4, 2) + rest), n, lambda c: c ^ 1)
    acc = mine.reshape((4, 2) + rest) + got
    via_up = col_send(acc[2, 0].astype(jnp.bfloat16), n, y_up).astype(jnp.float32)
    via_down = col_send(acc[2, 1].astype(jnp.bfloat16), n, y_down).astype(jnp.float32)
    to_up = jnp.stack([acc[1, 0] + via_up, acc[1, 1]]).astype(jnp.bfloat16)
    to_down = jnp.stack([acc[3, 0], acc[3, 1] + via_down]).astype(jnp.bfloat16)
    total = (
        acc[0]
        + col_send(to_up, n, y_up).astype(jnp.float32)
        + col_send(to_down, n, y_down).astype(jnp.float32)
    )
    return total[0] + col_send(total[1].astype(jnp.bfloat16), n, lambda c: c ^ 2).astype(jnp.float32)


def gather_col(own, n):
    pair = jnp.stack([own, col_send(own, n, lambda c: c ^ 2)])
    from_below = col_send(pair, n, y_up)
    from_above = col_send(pair, n, y_down)
    two_away = jnp.stack([col_send(from_above[0], n, y_down), col_send(from_below[1], n, y_up)])
    quad = jnp.stack([pair, from_above, two_away, from_below])
    rows = (8 * own.shape[0],) + own.shape[1:]
    return quad.reshape(rows), col_send(quad, n, lambda c: c ^ 1).reshape(rows)


def place_kernel(row_offset, slot_ref, adj_ref, dense_ref, dense_t_ref):
    row = pl.program_id(0) + row_offset
    col_total = dense_ref.shape[1] // adj_ref.shape[-1]
    size = adj_ref.shape[-1]
    for col in range(col_total):
        slot = slot_ref[row * col_total + col]
        tile = adj_ref[jnp.maximum(slot, 0)]
        tile = jnp.where(slot >= 0, tile, jnp.zeros_like(tile))
        dense_ref[:, col * size : (col + 1) * size] = tile
        dense_t_ref[col * size : (col + 1) * size, :] = tile.T


def place_rows(slot_of, tile_data, row_offset, row_count, col_total):
    slot_total, size, _ = tile_data.shape
    return pl.pallas_call(
        functools.partial(place_kernel, row_offset),
        grid_spec=pltpu.PrefetchScalarGridSpec(
            num_scalar_prefetch=1,
            grid=(row_count,),
            in_specs=[pl.BlockSpec((slot_total, size, size), lambda r, slots: (0, 0, 0))],
            out_specs=[
                pl.BlockSpec((size, col_total * size), lambda r, slots: (r, 0)),
                pl.BlockSpec((col_total * size, size), lambda r, slots: (0, r)),
            ],
        ),
        out_shape=[
            jax.ShapeDtypeStruct((row_count * size, col_total * size), tile_data.dtype),
            jax.ShapeDtypeStruct((col_total * size, row_count * size), tile_data.dtype),
        ],
        compiler_params=pltpu.CompilerParams(vmem_limit_bytes=48 * 1024 * 1024),
        cost_estimate=pl.CostEstimate(
            flops=0,
            transcendentals=0,
            bytes_accessed=slot_total * size * size * 2 + 2 * row_count * col_total * size * size * 2,
        ),
    )(slot_of, tile_data)


def dense_blocks(tile_data, row_ids, col_ids, in_count, row_total, col_total):
    slot_total = tile_data.shape[0]
    slot_range = jnp.arange(slot_total, dtype=jnp.int32)
    pair_of = jnp.where(slot_range < in_count, row_ids * col_total + col_ids, -1)
    pair_range = jnp.arange(row_total * col_total, dtype=jnp.int32)
    slot_of = jnp.max(
        jnp.where(pair_range[:, None] == pair_of[None, :], slot_range[None, :], -1), axis=1
    )
    half = row_total // 2
    mine, mine_t = place_rows(slot_of, tile_data, 0, half, col_total)
    other, other_t = place_rows(slot_of, tile_data, half, half, col_total)
    return mine, other, mine_t, other_t


def gather_by_a2a(x, axis_name, n):
    spread = jnp.broadcast_to(x[None], (n,) + x.shape)
    return lax.all_to_all(spread, axis_name, 0, 0, tiled=False).reshape((n * x.shape[0],) + x.shape[1:])


def scatter_sum_by_a2a(x, axis_name, n, link_dtype):
    parts = x.astype(link_dtype).reshape((n, x.shape[0] // n) + x.shape[1:])
    got = lax.all_to_all(parts, axis_name, 0, 0, tiled=False)
    return jnp.sum(got.astype(jnp.float32), axis=0)


def all_sum_by_a2a(x, axis_names, n, scale):
    pad = (-x.shape[0]) % n
    parts = jnp.pad(x, (0, pad)).reshape(n, -1)
    got = lax.all_to_all(parts.astype(jnp.bfloat16), axis_names, 0, 0, tiled=False)
    mine = jnp.sum(got.astype(jnp.float32), axis=0) * scale
    back = lax.all_to_all(jnp.broadcast_to(mine[None], parts.shape), axis_names, 0, 0, tiled=False)
    return back.reshape(-1)[: x.shape[0]]


def slope_of(shifted, cotangent):
    sig = jax.nn.sigmoid(shifted)
    return (cotangent.astype(jnp.float32) * sig * (1.0 + shifted * (1.0 - sig))).astype(
        jnp.bfloat16
    )


def on_device_body(features, cotangent, weights, bias_term, adjacency, tile_rows, tile_cols, tile_count):
    tile_size = adjacency.shape[-1]
    slot_total = adjacency.shape[2]
    tile_data = adjacency.reshape(slot_total, tile_size, tile_size)
    row_ids = tile_rows.reshape(slot_total)
    col_ids = tile_cols.reshape(slot_total)
    in_count = tile_count.reshape(())
    n_row = lax.axis_size("row")
    n_col = lax.axis_size("col")
    own_rows = features.shape[0]
    own_blocks = own_rows // tile_size
    feat_width = features.shape[1]
    row_total = n_col * own_blocks
    col_total = n_row * own_blocks
    node_scale = 1.0 / math.sqrt(own_rows * n_row * n_col)

    me_col = lax.axis_index("col")
    rel_rows = relative_col(row_ids // own_blocks, me_col) * own_blocks + row_ids % own_blocks
    dense_mine, dense_other, dense_t_mine, dense_t_other = dense_blocks(tile_data, rel_rows, col_ids, in_count, row_total, col_total)

    projected = jnp.dot(features, weights, preferred_element_type=jnp.float32).astype(jnp.bfloat16)
    gathered = gather_by_a2a(projected, "row", n_row)
    other_rows = jnp.dot(dense_other, gathered, preferred_element_type=jnp.float32)
    mine_rows = lax.optimization_barrier(
        jnp.dot(dense_mine, gathered, preferred_element_type=jnp.float32)
    )
    bias_row = bias_term[None, :]
    shifted = (
        scatter_sum_col(
            mine_rows.reshape(n_col // 2, own_rows, feat_width),
            other_rows.reshape(n_col // 2, own_rows, feat_width),
            n_col,
        )
        + bias_row
    )
    slope_own = slope_of(shifted, cotangent)
    slope_mine, slope_other = gather_col(slope_own, n_col)
    activated = jax.nn.silu(shifted).astype(jnp.bfloat16)
    bias_part = jnp.sum(slope_own.astype(jnp.float32), axis=0)
    cols_mine = lax.optimization_barrier(
        jnp.dot(dense_t_mine, slope_mine, preferred_element_type=jnp.float32)
    )
    partial_cols = cols_mine + jnp.dot(dense_t_other, slope_other, preferred_element_type=jnp.float32)
    back = scatter_sum_by_a2a(partial_cols, "row", n_row, jnp.bfloat16).astype(jnp.bfloat16)
    grad_input = lax.dot_general(
        back, weights, (((1,), (1,)), ((), ())), preferred_element_type=jnp.float32
    ).astype(jnp.bfloat16)
    weight_part = lax.dot_general(
        features, back, (((0,), (0,)), ((), ())), preferred_element_type=jnp.float32
    )
    joined = jnp.concatenate([weight_part.reshape(-1), bias_part])
    joined = all_sum_by_a2a(joined, ("row", "col"), n_row * n_col, node_scale)
    weight_sum = joined[: feat_width * feat_width].reshape(feat_width, feat_width)
    bias_sum = joined[feat_width * feat_width :]
    return (activated, grad_input, weight_sum, bias_sum)


def solution(mesh):
    return sharded(mesh)


def sharded(mesh):
    return jax.shard_map(
        on_device_body,
        mesh=mesh,
        in_specs=(
            P(("row", "col"), None),
            P(("row", "col"), None),
            P(),
            P(),
            P("row", "col", None, None, None),
            P("row", "col", None),
            P("row", "col", None),
            P("row", "col"),
        ),
        out_specs=(P(("row", "col"), None), P(("row", "col"), None), P(), P()),
        check_vma=False,
    )
```

```python
import functools
import math

import jax
import jax.numpy as jnp
from jax import lax
from jax.experimental import pallas as pl
from jax.experimental.pallas import tpu as pltpu
from jax.sharding import PartitionSpec as P


def col_parts(c):
    return c // 4, (c // 2) % 2, c % 2


def relative_col(c2, me):
    y2, x2, k2 = col_parts(c2)
    y1, x1, k1 = col_parts(me)
    return (k2 ^ k1) * 8 + ((y2 - y1) % 4) * 2 + (x2 ^ x1)


def col_send(x, n, move):
    return lax.ppermute(x, "col", [(c, move(c)) for c in range(n)])


def y_up(c):
    return ((c // 4 + 1) % 4) * 4 + c % 4


def y_down(c):
    return ((c // 4 + 3) % 4) * 4 + c % 4


def scatter_sum_col(mine, other, n):
    rest = mine.shape[1:]
    got = col_send(other.reshape((4, 2) + rest), n, lambda c: c ^ 1)
    acc = mine.reshape((4, 2) + rest) + got
    via_up = col_send(acc[2, 0].astype(jnp.bfloat16), n, y_up).astype(jnp.float32)
    via_down = col_send(acc[2, 1].astype(jnp.bfloat16), n, y_down).astype(jnp.float32)
    to_up = jnp.stack([acc[1, 0] + via_up, acc[1, 1]]).astype(jnp.bfloat16)
    to_down = jnp.stack([acc[3, 0], acc[3, 1] + via_down]).astype(jnp.bfloat16)
    total = (
        acc[0]
        + col_send(to_up, n, y_up).astype(jnp.float32)
        + col_send(to_down, n, y_down).astype(jnp.float32)
    )
    return total[0] + col_send(total[1].astype(jnp.bfloat16), n, lambda c: c ^ 2).astype(jnp.float32)


def gather_col(own, n):
    pair = jnp.stack([own, col_send(own, n, lambda c: c ^ 2)])
    from_below = col_send(pair, n, y_up)
    from_above = col_send(pair, n, y_down)
    two_away = jnp.stack([col_send(from_above[0], n, y_down), col_send(from_below[1], n, y_up)])
    quad = jnp.stack([pair, from_above, two_away, from_below])
    rows = (8 * own.shape[0],) + own.shape[1:]
    return quad.reshape(rows), col_send(quad, n, lambda c: c ^ 1).reshape(rows)


def place_kernel(row_offset, slot_ref, adj_ref, dense_ref):
    row = pl.program_id(0) + row_offset
    col_total = dense_ref.shape[1] // adj_ref.shape[-1]
    size = adj_ref.shape[-1]
    for col in range(col_total):
        slot = slot_ref[row * col_total + col]
        tile = adj_ref[jnp.maximum(slot, 0)]
        tile = jnp.where(slot >= 0, tile, jnp.zeros_like(tile))
        dense_ref[:, col * size : (col + 1) * size] = tile


def place_rows(slot_of, tile_data, row_offset, row_count, col_total):
    slot_total, size, _ = tile_data.shape
    return pl.pallas_call(
        functools.partial(place_kernel, row_offset),
        grid_spec=pltpu.PrefetchScalarGridSpec(
            num_scalar_prefetch=1,
            grid=(row_count,),
            in_specs=[pl.BlockSpec((slot_total, size, size), lambda r, slots: (0, 0, 0))],
            out_specs=pl.BlockSpec((size, col_total * size), lambda r, slots: (r, 0)),
        ),
        out_shape=jax.ShapeDtypeStruct((row_count * size, col_total * size), tile_data.dtype),
        compiler_params=pltpu.CompilerParams(vmem_limit_bytes=48 * 1024 * 1024),
        cost_estimate=pl.CostEstimate(
            flops=0,
            transcendentals=0,
            bytes_accessed=slot_total * size * size * 2 + row_count * col_total * size * size * 2,
        ),
    )(slot_of, tile_data)


def dense_blocks(tile_data, row_ids, col_ids, in_count, row_total, col_total):
    slot_total = tile_data.shape[0]
    slot_range = jnp.arange(slot_total, dtype=jnp.int32)
    pair_of = jnp.where(slot_range < in_count, row_ids * col_total + col_ids, -1)
    pair_range = jnp.arange(row_total * col_total, dtype=jnp.int32)
    slot_of = jnp.max(
        jnp.where(pair_range[:, None] == pair_of[None, :], slot_range[None, :], -1), axis=1
    )
    half = row_total // 2
    mine = place_rows(slot_of, tile_data, 0, half, col_total)
    other = place_rows(slot_of, tile_data, half, half, col_total)
    return mine, other


def gather_by_a2a(x, axis_name, n):
    spread = jnp.broadcast_to(x[None], (n,) + x.shape)
    return lax.all_to_all(spread, axis_name, 0, 0, tiled=False).reshape((n * x.shape[0],) + x.shape[1:])


def scatter_sum_by_a2a(x, axis_name, n, link_dtype):
    parts = x.astype(link_dtype).reshape((n, x.shape[0] // n) + x.shape[1:])
    got = lax.all_to_all(parts, axis_name, 0, 0, tiled=False)
    return jnp.sum(got.astype(jnp.float32), axis=0)


def all_sum_by_a2a(x, axis_names, n, scale):
    pad = (-x.shape[0]) % n
    parts = jnp.pad(x, (0, pad)).reshape(n, -1)
    got = lax.all_to_all(parts, axis_names, 0, 0, tiled=False)
    mine = jnp.sum(got, axis=0) * scale
    back = lax.all_to_all(jnp.broadcast_to(mine[None], parts.shape), axis_names, 0, 0, tiled=False)
    return back.reshape(-1)[: x.shape[0]]


def slope_of(shifted, cotangent):
    sig = jax.nn.sigmoid(shifted)
    return (cotangent.astype(jnp.float32) * sig * (1.0 + shifted * (1.0 - sig))).astype(
        jnp.bfloat16
    )


def on_device_body(features, cotangent, weights, bias_term, adjacency, tile_rows, tile_cols, tile_count):
    tile_size = adjacency.shape[-1]
    slot_total = adjacency.shape[2]
    tile_data = adjacency.reshape(slot_total, tile_size, tile_size)
    row_ids = tile_rows.reshape(slot_total)
    col_ids = tile_cols.reshape(slot_total)
    in_count = tile_count.reshape(())
    n_row = lax.axis_size("row")
    n_col = lax.axis_size("col")
    own_rows = features.shape[0]
    own_blocks = own_rows // tile_size
    feat_width = features.shape[1]
    row_total = n_col * own_blocks
    col_total = n_row * own_blocks
    node_scale = 1.0 / math.sqrt(own_rows * n_row * n_col)

    me_col = lax.axis_index("col")
    rel_rows = relative_col(row_ids // own_blocks, me_col) * own_blocks + row_ids % own_blocks
    dense_mine, dense_other = dense_blocks(tile_data, rel_rows, col_ids, in_count, row_total, col_total)

    projected = jnp.dot(features, weights, preferred_element_type=jnp.float32).astype(jnp.bfloat16)
    gathered = gather_by_a2a(projected, "row", n_row)
    other_rows = jnp.dot(dense_other, gathered, preferred_element_type=jnp.float32)
    mine_rows = lax.optimization_barrier(
        jnp.dot(dense_mine, gathered, preferred_element_type=jnp.float32)
    )
    bias_row = bias_term[None, :]
    shifted = (
        scatter_sum_col(
            mine_rows.reshape(n_col // 2, own_rows, feat_width),
            other_rows.reshape(n_col // 2, own_rows, feat_width),
            n_col,
        )
        + bias_row
    )
    slope_own = slope_of(shifted, cotangent)
    slope_mine, slope_other = gather_col(slope_own, n_col)
    activated = jax.nn.silu(shifted).astype(jnp.bfloat16)
    bias_part = jnp.sum(slope_own.astype(jnp.float32), axis=0)
    cols_mine = lax.optimization_barrier(
        lax.dot_general(
            dense_mine, slope_mine, (((0,), (0,)), ((), ())), preferred_element_type=jnp.float32
        )
    )
    partial_cols = cols_mine + lax.dot_general(
        dense_other, slope_other, (((0,), (0,)), ((), ())), preferred_element_type=jnp.float32
    )
    back = scatter_sum_by_a2a(partial_cols, "row", n_row, jnp.bfloat16).astype(jnp.bfloat16)
    grad_input = lax.dot_general(
        back, weights, (((1,), (1,)), ((), ())), preferred_element_type=jnp.float32
    ).astype(jnp.bfloat16)
    weight_part = lax.dot_general(
        features, back, (((0,), (0,)), ((), ())), preferred_element_type=jnp.float32
    )
    joined = jnp.concatenate([weight_part.reshape(-1), bias_part])
    joined = all_sum_by_a2a(joined, ("row", "col"), n_row * n_col, node_scale)
    weight_sum = joined[: feat_width * feat_width].reshape(feat_width, feat_width)
    bias_sum = joined[feat_width * feat_width :]
    return (activated, grad_input, weight_sum, bias_sum)


def solution(mesh):
    return sharded(mesh)


def sharded(mesh):
    return jax.shard_map(
        on_device_body,
        mesh=mesh,
        in_specs=(
            P(("row", "col"), None),
            P(("row", "col"), None),
            P(),
            P(),
            P("row", "col", None, None, None),
            P("row", "col", None),
            P("row", "col", None),
            P("row", "col"),
        ),
        out_specs=(P(("row", "col"), None), P(("row", "col"), None), P(), P()),
        check_vma=False,
    )
```
